512 devices in a mesh: dom: 128 (over z, y, core), feat: 4 (over x).
Axes of the slice: x: 4, y: 8, z: 8, core: 2. Of those that a mesh axis runs over, the one named last changes fastest.
Arguments:
- node_feats: bfloat16 [256, 262144], P('feat', 'dom'), may hold values from -6 to 6
- weight: bfloat16 [256, 256], P(None, 'feat'), may hold values from -0.375 to 0.375
- bias_vec: bfloat16 [256], P('feat'), may hold values from -3 to 3
- adj_tiles: bfloat16 [12288, 128, 128], P('dom'), may hold values from -0.25 to 0.25
- tile_row: int32 [12288], P('dom'), may hold values from 0 to 15, as said below
- tile_col: int32 [12288], P('dom'), may hold values from 0 to 143, as said below
- tile_count: int32 [128], P('dom'), may hold values from 58 to 96
- send_block: int32 [16384], P('dom'), may hold values from 0 to 15, as said below
- cotangent: bfloat16 [256, 262144], P('feat', 'dom'), may hold values from -6 to 6
Outputs:
- activations: bfloat16 [256, 262144], P('feat', 'dom')
- grad_input: bfloat16 [256, 262144], P('feat', 'dom')
- grad_weight: float32 [256, 256], P(None, 'feat')
- grad_bias: float32 [256], P('feat')
The draws below stay inside these ranges and needn't reach their ends.
Inputs may be any that keep to these rules, and one draw needn't show every extreme that they name: `tile_row`: entries past a partition's tile_count are padding, of the same range. `tile_col`: among a partition's valid entries, each peer's halo slot 16 + q is named at most once, and a partition's own slot never. `send_block`: entry q * 128 + p is the local block that partition q sends to partition p; it is defined for every pair.
All inputs are finite; a program needn't handle non-finite values.
Results may differ from the reference program's by a relative error of at most 0.0064.
Values may be sent and summed in bfloat16 or wider, within the bound.
No kernel may reach another device: no remote copies, remote signals or barrier semaphores. Data moves between devices by JAX's collectives and lax.ppermute only.
A program may use at most 64 MiB of HBM per device.

```python
import math
import jax
import jax.numpy as jnp
from jax import lax

D = 256
BLOCK = 128
BLK_DEV = 16
TILE_DEV = 96
NODES = 262144
N_DOM = 128


def graph_lists(key):
    base = jax.random.fold_in(key, 17)
    subkeys = jax.random.split(base, 9)
    peer_ids = jnp.arange(N_DOM, dtype=jnp.int32)
    fewest = N_DOM // 3
    most_far = N_DOM // 2
    far_count = jax.random.randint(subkeys[0], (N_DOM,), fewest, most_far + 1)
    near_count = jax.random.randint(subkeys[1], (N_DOM,), 0, BLK_DEV + 1)
    busiest = jax.random.randint(subkeys[2], (), 0, N_DOM)
    lightest = (busiest + 1 + jax.random.randint(subkeys[3], (), 0, N_DOM - 1)) % N_DOM
    far_count = jnp.where(peer_ids == busiest, most_far, jnp.where(peer_ids == lightest, fewest, far_count))
    near_count = jnp.where(peer_ids == busiest, BLK_DEV, jnp.where(peer_ids == lightest, 0, near_count))
    scores = jax.random.randint(subkeys[4], (N_DOM, N_DOM), 0, 1 << 20) * N_DOM + peer_ids[None, :]
    scores = jnp.where(peer_ids[None, :] == peer_ids[:, None], (1 << 20) * N_DOM + N_DOM, scores)
    ranks = jnp.argsort(jnp.argsort(scores, axis=1), axis=1)
    filled = ranks < far_count[:, None]
    order = jnp.argsort(jnp.where(filled, 0, N_DOM) + peer_ids[None, :], axis=1).astype(jnp.int32)
    position = jnp.arange(TILE_DEV, dtype=jnp.int32)[None, :]
    slot_rank = position - BLK_DEV - near_count[:, None]
    far_peer = jnp.take_along_axis(order, jnp.clip(slot_rank, 0, N_DOM - 1), axis=1)
    rand_row = jax.random.randint(subkeys[5], (N_DOM, TILE_DEV), 0, BLK_DEV)
    rand_near = jax.random.randint(subkeys[6], (N_DOM, TILE_DEV), 0, BLK_DEV)
    rand_pad = jax.random.randint(subkeys[7], (N_DOM, TILE_DEV), 0, BLK_DEV + N_DOM)
    is_diag = position < BLK_DEV
    is_near = jnp.logical_and(jnp.logical_not(is_diag), slot_rank < 0)
    is_far = jnp.logical_and(slot_rank >= 0, slot_rank < far_count[:, None])
    row_ids = jnp.where(is_diag, position, rand_row)
    col_ids = jnp.where(is_diag, position, jnp.where(is_near, rand_near, jnp.where(is_far, BLK_DEV + far_peer, rand_pad)))
    counts = BLK_DEV + near_count + far_count
    sends = jax.random.randint(subkeys[8], (N_DOM, N_DOM), 0, BLK_DEV)
    return (row_ids.astype(jnp.int32), col_ids.astype(jnp.int32), counts.astype(jnp.int32), sends.astype(jnp.int32))


def draw_tile_row(key, part):
    return graph_lists(key)[0].reshape(-1)


def draw_tile_col(key, part):
    return graph_lists(key)[1].reshape(-1)


def draw_tile_count(key, part):
    return graph_lists(key)[2]


def draw_send_block(key, part):
    return graph_lists(key)[3].reshape(-1)


def block_levels(key, dims, shards, low, high):
    level, own = 1.0, jax.random.fold_in(key, 6)
    for dim, shards_of in shards:
        steps = jnp.exp(jax.random.uniform(jax.random.fold_in(own, dim), (shards_of,), jnp.float32, low / len(shards), high / len(shards)))
        level = level * jnp.repeat(steps, dims[dim] // shards_of).reshape([-1 if axis == dim else 1 for axis in range(len(dims))])
    return level


def scatter_about(stream_key, dims, scale, limit, shards=(), kind=jnp.bfloat16):
    values = scale * jax.random.normal(stream_key, dims, jnp.float32)
    if shards:
        values = values * block_levels(stream_key, dims, shards, -0.22, 0.18)
    return jnp.clip(values, -limit, limit).astype(kind)


def setup_inputs(seed: int = 0) -> dict:
    keys = jax.random.split(jax.random.key(seed), 10)
    return {
        "node_feats": scatter_about(keys[0], (D, NODES), 1.0, 6.0, ((0, 4), (1, 128))),
        "weight": scatter_about(keys[1], (D, D), D ** -0.5, 0.375, ((1, 4),)),
        "bias_vec": scatter_about(keys[2], (D,), 0.5, 3.0, ((0, 4),)),
        "adj_tiles": scatter_about(keys[3], (N_DOM * TILE_DEV, BLOCK, BLOCK), (4 * BLOCK) ** -0.5, 0.25, ((0, 128),)),
        "tile_row": draw_tile_row(jax.random.fold_in(keys[9], 71), 0),
        "tile_col": draw_tile_col(jax.random.fold_in(keys[9], 71), 0),
        "tile_count": draw_tile_count(jax.random.fold_in(keys[9], 71), 0),
        "send_block": draw_send_block(jax.random.fold_in(keys[9], 71), 0),
        "cotangent": scatter_about(keys[8], (D, NODES), 1.0, 6.0, ((0, 4), (1, 128))),
    }


def smooth_gate(values):
    return jax.nn.gelu(values, approximate=True)

def column_blocks(partition, col_ids, send_block):
    peer_ids = jnp.clip(col_ids - BLK_DEV, 0, N_DOM - 1).astype(jnp.int32)
    far_block = peer_ids * BLK_DEV + send_block[(peer_ids * N_DOM + partition).astype(jnp.int32)]
    return jnp.where(col_ids < BLK_DEV, partition * BLK_DEV + col_ids, far_block).astype(jnp.int32)

def reference(node_feats, weight, bias_vec, adj_tiles, tile_row, tile_col, tile_count, send_block, cotangent):
    hidden = jnp.dot(weight.T, node_feats, preferred_element_type=jnp.float32).astype(jnp.bfloat16)
    hid_blocks = hidden.reshape(D, N_DOM * BLK_DEV, BLOCK)
    slot_ids = jnp.arange(TILE_DEV, dtype=jnp.int32)
    block_ids = jnp.arange(BLK_DEV, dtype=jnp.int32)

    def part_lists(partition):
        offset = (partition * TILE_DEV).astype(jnp.int32)
        tile_vals = lax.dynamic_slice_in_dim(adj_tiles, offset, TILE_DEV, 0).astype(jnp.float32)
        row_ids = lax.dynamic_slice_in_dim(tile_row, offset, TILE_DEV, 0).astype(jnp.int32)
        col_ids = lax.dynamic_slice_in_dim(tile_col, offset, TILE_DEV, 0).astype(jnp.int32)
        live_mask = (slot_ids < tile_count[partition]).astype(jnp.float32)
        return (tile_vals, row_ids, col_ids, live_mask)

    def forward_part(partition):
        tile_vals, row_ids, col_ids, live_mask = part_lists(partition)
        picked = jnp.take(hid_blocks, column_blocks(partition, col_ids, send_block), axis=1).astype(jnp.float32)
        products = jnp.einsum('otb,tab->ota', picked, tile_vals)
        row_place = (row_ids[:, None] == block_ids[None, :]).astype(jnp.float32) * live_mask[:, None]
        return jnp.einsum('ota,tr->ora', products, row_place, precision=lax.Precision.HIGHEST)
    per_part = lax.map(forward_part, jnp.arange(N_DOM, dtype=jnp.int32))
    summed = jnp.transpose(per_part, (1, 0, 2, 3)).reshape(D, NODES)
    preact = summed + bias_vec.astype(jnp.float32)[:, None]
    activated, pullback = jax.vjp(smooth_gate, preact)
    grad_pre = pullback(cotangent.astype(jnp.float32))[0]
    grad_low = grad_pre.astype(jnp.bfloat16)
    grad_blocks = grad_low.reshape(D, N_DOM * BLK_DEV, BLOCK)

    def backward_part(running, partition):
        tile_vals, row_ids, col_ids, live_mask = part_lists(partition)
        picked = jnp.take(grad_blocks, (partition * BLK_DEV + row_ids).astype(jnp.int32), axis=1).astype(jnp.float32)
        products = jnp.einsum('ota,tab->otb', picked, tile_vals) * live_mask[None, :, None]
        return (running.at[:, column_blocks(partition, col_ids, send_block), :].add(products), None)
    start_sum = jnp.zeros((D, N_DOM * BLK_DEV, BLOCK), jnp.float32)
    grad_sum, _ = lax.scan(backward_part, start_sum, jnp.arange(N_DOM, dtype=jnp.int32))
    grad_hidden = grad_sum.reshape(D, NODES).astype(jnp.bfloat16)
    norm_scale = 1.0 / math.sqrt(NODES)
    grad_weight = jnp.dot(node_feats, grad_hidden.T, preferred_element_type=jnp.float32) * norm_scale
    grad_bias = lax.optimization_barrier(jnp.sum(grad_pre, axis=1)) * norm_scale
    grad_input = jnp.dot(weight, grad_hidden, preferred_element_type=jnp.float32).astype(jnp.bfloat16)
    return (activated.astype(jnp.bfloat16), grad_input, grad_weight, grad_bias)
```

```python
import math

import jax
import jax.numpy as jnp
from jax import lax
from jax.sharding import PartitionSpec as P


def smooth_gate(values):
    return jax.nn.gelu(values, approximate=True)


def butterfly_sum(values, axis, size):
    step = 1
    while step < size:
        pairs = [(i, i ^ step) for i in range(size)]
        values = values + lax.ppermute(values, axis, pairs)
        step *= 2
    return values


def per_device(
    node_feats, weight, bias_vec, adj_tiles, tile_row, tile_col, tile_count, send_block, cotangent
):
    feat_rows, node_rows = node_feats.shape
    tile_slots = adj_tiles.shape[0]
    tile_size = adj_tiles.shape[1]
    blocks = node_rows // tile_size
    domains = lax.axis_size("dom")
    whole = lax.all_gather(node_feats, "feat", axis=0, tiled=True)
    hidden = lax.dot_general(
        weight, whole, (((0,), (0,)), ((), ())), preferred_element_type=jnp.float32
    ).astype(jnp.bfloat16)
    hid_blocks = hidden.reshape(feat_rows, blocks, tile_size)
    outgoing = jnp.take(hid_blocks, send_block, axis=1)
    incoming = lax.all_to_all(outgoing, "dom", split_axis=1, concat_axis=1, tiled=True)
    sources = jnp.concatenate([hid_blocks, incoming], axis=1)
    live_tiles = jnp.arange(tile_slots) < tile_count[0]
    live_float = live_tiles.astype(jnp.float32)
    row_place = (tile_row[:, None] == jnp.arange(blocks)[None, :]).astype(jnp.float32) * live_float[
        :, None
    ]
    picked = jnp.take(sources, tile_col, axis=1)
    products = jnp.einsum("otb,tab->ota", picked, adj_tiles, preferred_element_type=jnp.float32)
    summed = jnp.einsum(
        "ota,tr->ora", products, row_place, precision=lax.Precision.HIGHEST
    ).reshape(feat_rows, node_rows)
    preact = summed + bias_vec.astype(jnp.float32)[:, None]
    activated, pullback = jax.vjp(smooth_gate, preact)
    grad_pre = pullback(cotangent.astype(jnp.float32))[0]
    grad_low = grad_pre.astype(jnp.bfloat16)
    grad_blocks = grad_low.reshape(feat_rows, blocks, tile_size)
    rows_picked = jnp.take(grad_blocks, tile_row, axis=1)
    backward = jnp.einsum(
        "ota,tab->otb", rows_picked, adj_tiles, preferred_element_type=jnp.float32
    )
    src_place = (tile_col[:, None] == jnp.arange(blocks)[None, :]).astype(
        jnp.float32
    ) * live_float[:, None]
    recv_place = (send_block[:, None] == jnp.arange(blocks)[None, :]).astype(jnp.float32)
    own_sum = jnp.einsum(
        "otb,tr->orb", backward, src_place, precision=lax.Precision.HIGHEST
    )
    slot_hit = jnp.logical_and(
        tile_col[:, None] == blocks + jnp.arange(domains)[None, :], live_tiles[:, None]
    )
    hit_tile = jnp.sum(jnp.where(slot_hit, jnp.arange(tile_slots)[:, None], 0), axis=0)
    has_hit = jnp.any(slot_hit, axis=0)
    out_parts = jnp.where(
        has_hit[None, :, None], jnp.take(backward, hit_tile, axis=1), 0.0
    )
    in_parts = lax.all_to_all(out_parts, "dom", split_axis=1, concat_axis=1, tiled=True)
    grad_sum = own_sum + jnp.einsum(
        "oqb,qr->orb", in_parts, recv_place, precision=lax.Precision.HIGHEST
    )
    grad_hidden = grad_sum.reshape(feat_rows, node_rows).astype(jnp.bfloat16)
    norm_scale = 1.0 / math.sqrt(domains * node_rows)
    weight_part = lax.dot_general(
        whole, grad_hidden, (((1,), (1,)), ((), ())), preferred_element_type=jnp.float32
    )
    bias_part = jnp.sum(grad_pre, axis=1)
    packed = jnp.concatenate([weight_part, bias_part[None, :]], axis=0)
    packed = butterfly_sum(packed, "dom", domains)
    grad_weight = packed[:-1] * norm_scale
    grad_bias = packed[-1] * norm_scale
    full_weight, all_grad = (
        lax.all_gather(weight, "feat", axis=1, tiled=True),
        lax.all_gather(grad_hidden, "feat", axis=0, tiled=True),
    )
    my_rows = lax.dynamic_slice_in_dim(
        full_weight, lax.axis_index("feat") * feat_rows, feat_rows, 0
    )
    grad_input = jnp.dot(my_rows, all_grad, preferred_element_type=jnp.float32).astype(jnp.bfloat16)
    return (activated.astype(jnp.bfloat16), grad_input, grad_weight, grad_bias)


def solution(mesh):
    placed = (
        P("feat", "dom"),
        P(None, "feat"),
        P("feat"),
        P("dom", None, None),
        P("dom"),
        P("dom"),
        P("dom"),
        P("dom"),
        P("feat", "dom"),
    )
    return jax.shard_map(
        per_device,
        mesh=mesh,
        in_specs=placed,
        out_specs=(P("feat", "dom"), P("feat", "dom"), P(None, "feat"), P("feat")),
        check_vma=False,
    )
```

```python
import math

import jax
import jax.numpy as jnp
from jax import lax
from jax.sharding import PartitionSpec as P


def smooth_gate(values):
    return jax.nn.gelu(values, approximate=True)


def group_stack(values, axis, size, stride, count):
    received = [values]
    for offset in range(1, count):
        pairs = [(i, i ^ (offset * stride)) for i in range(size)]
        received.append(lax.ppermute(values, axis, pairs))
    stacked = jnp.stack(received)
    mine = (lax.axis_index(axis) // stride) % count
    return jnp.take(stacked, mine ^ jnp.arange(count), axis=0)


def group_sum(values, axis, size, stride, count):
    return jnp.sum(group_stack(values, axis, size, stride, count), axis=0)


def per_device(
    node_feats, weight, bias_vec, adj_tiles, tile_row, tile_col, tile_count, send_block, cotangent
):
    feat_rows, node_rows = node_feats.shape
    tile_slots = adj_tiles.shape[0]
    tile_size = adj_tiles.shape[1]
    blocks = node_rows // tile_size
    domains = lax.axis_size("dom")
    parts = lax.axis_size("feat")
    whole = group_stack(node_feats, "feat", parts, 1, parts).reshape(parts * feat_rows, node_rows)
    hidden = lax.dot_general(
        weight, whole, (((0,), (0,)), ((), ())), preferred_element_type=jnp.float32
    ).astype(jnp.bfloat16)
    hid_blocks = hidden.reshape(feat_rows, blocks, tile_size)
    outgoing = jnp.take(hid_blocks, send_block, axis=1)
    incoming = lax.all_to_all(outgoing, "dom", split_axis=1, concat_axis=1, tiled=True)
    sources = jnp.concatenate([hid_blocks, incoming], axis=1)
    live_tiles = jnp.arange(tile_slots) < tile_count[0]
    live_float = live_tiles.astype(jnp.float32)
    row_place = (tile_row[:, None] == jnp.arange(blocks)[None, :]).astype(jnp.float32) * live_float[
        :, None
    ]
    picked = jnp.take(sources, tile_col, axis=1)
    products = jnp.einsum("otb,tab->ota", picked, adj_tiles, preferred_element_type=jnp.float32)
    summed = jnp.einsum(
        "ota,tr->ora", products, row_place, precision=lax.Precision.HIGHEST
    ).reshape(feat_rows, node_rows)
    preact = summed + bias_vec.astype(jnp.float32)[:, None]
    activated, pullback = jax.vjp(smooth_gate, preact)
    grad_pre = pullback(cotangent.astype(jnp.float32))[0]
    grad_low = grad_pre.astype(jnp.bfloat16)
    grad_blocks = grad_low.reshape(feat_rows, blocks, tile_size)
    rows_picked = jnp.take(grad_blocks, tile_row, axis=1)
    backward = jnp.einsum(
        "ota,tab->otb", rows_picked, adj_tiles, preferred_element_type=jnp.float32
    )
    src_place = (tile_col[:, None] == jnp.arange(blocks)[None, :]).astype(
        jnp.float32
    ) * live_float[:, None]
    recv_place = (send_block[:, None] == jnp.arange(blocks)[None, :]).astype(jnp.float32)
    own_sum = jnp.einsum(
        "otb,tr->orb", backward, src_place, precision=lax.Precision.HIGHEST
    )
    slot_hit = jnp.logical_and(
        tile_col[:, None] == blocks + jnp.arange(domains)[None, :], live_tiles[:, None]
    )
    hit_tile = jnp.sum(jnp.where(slot_hit, jnp.arange(tile_slots)[:, None], 0), axis=0)
    has_hit = jnp.any(slot_hit, axis=0)
    out_parts = jnp.where(
        has_hit[None, :, None], jnp.take(backward, hit_tile, axis=1), 0.0
    )
    in_parts = lax.all_to_all(out_parts, "dom", split_axis=1, concat_axis=1, tiled=True)
    grad_sum = own_sum + jnp.einsum(
        "oqb,qr->orb", in_parts, recv_place, precision=lax.Precision.HIGHEST
    )
    grad_hidden = grad_sum.reshape(feat_rows, node_rows).astype(jnp.bfloat16)
    norm_scale = 1.0 / math.sqrt(domains * node_rows)
    weight_part = lax.dot_general(
        whole, grad_hidden, (((1,), (1,)), ((), ())), preferred_element_type=jnp.float32
    )
    bias_part = jnp.sum(grad_pre, axis=1)
    packed = jnp.concatenate([weight_part, bias_part[None, :]], axis=0)
    low = 16 if domains % 16 == 0 else 1
    packed = group_sum(packed, "dom", domains, 1, low)
    packed = group_sum(packed, "dom", domains, low, domains // low)
    grad_weight = packed[:-1] * norm_scale
    grad_bias = packed[-1] * norm_scale
    full_weight = jnp.concatenate(list(group_stack(weight, "feat", parts, 1, parts)), axis=1)
    all_grad = group_stack(grad_hidden, "feat", parts, 1, parts).reshape(parts * feat_rows, node_rows)
    my_rows = lax.dynamic_slice_in_dim(
        full_weight, lax.axis_index("feat") * feat_rows, feat_rows, 0
    )
    grad_input = jnp.dot(my_rows, all_grad, preferred_element_type=jnp.float32).astype(jnp.bfloat16)
    return (activated.astype(jnp.bfloat16), grad_input, grad_weight, grad_bias)


def solution(mesh):
    placed = (
        P("feat", "dom"),
        P(None, "feat"),
        P("feat"),
        P("dom", None, None),
        P("dom"),
        P("dom"),
        P("dom"),
        P("dom"),
        P("feat", "dom"),
    )
    return jax.shard_map(
        per_device,
        mesh=mesh,
        in_specs=placed,
        out_specs=(P("feat", "dom"), P("feat", "dom"), P(None, "feat"), P("feat")),
        check_vma=False,
    )
```

```python
import math

import jax
import jax.numpy as jnp
from jax import lax
from jax.sharding import PartitionSpec as P


def smooth_gate(values):
    return jax.nn.gelu(values, approximate=True)


def group_stack(values, axis, size, stride, count):
    received = [values]
    for offset in range(1, count):
        pairs = [(i, i ^ (offset * stride)) for i in range(size)]
        received.append(lax.ppermute(values, axis, pairs))
    stacked = jnp.stack(received)
    mine = (lax.axis_index(axis) // stride) % count
    return jnp.take(stacked, mine ^ jnp.arange(count), axis=0)


def scatter_gather_sum(values, axis, size):
    rows, cols = values.shape
    chunk = -(-rows // size)
    padded = jnp.pad(values, ((0, chunk * size - rows), (0, 0))).reshape(size, chunk, cols)
    gathered = lax.all_to_all(padded, axis, 0, 0, tiled=True)
    reduced = jnp.sum(gathered, axis=0)
    spread = jnp.broadcast_to(reduced[None], (size, chunk, cols))
    total = lax.all_to_all(spread, axis, 0, 0, tiled=True)
    return total.reshape(size * chunk, cols)[:rows]


def per_device(
    node_feats, weight, bias_vec, adj_tiles, tile_row, tile_col, tile_count, send_block, cotangent
):
    feat_rows, node_rows = node_feats.shape
    tile_slots = adj_tiles.shape[0]
    tile_size = adj_tiles.shape[1]
    blocks = node_rows // tile_size
    domains = lax.axis_size("dom")
    parts = lax.axis_size("feat")
    whole = group_stack(node_feats, "feat", parts, 1, parts).reshape(parts * feat_rows, node_rows)
    hidden = lax.dot_general(
        weight, whole, (((0,), (0,)), ((), ())), preferred_element_type=jnp.float32
    ).astype(jnp.bfloat16)
    hid_blocks = hidden.reshape(feat_rows, blocks, tile_size)
    outgoing = jnp.take(hid_blocks, send_block, axis=1)
    incoming = lax.all_to_all(outgoing, "dom", split_axis=1, concat_axis=1, tiled=True)
    sources = jnp.concatenate([hid_blocks, incoming], axis=1)
    live_tiles = jnp.arange(tile_slots) < tile_count[0]
    live_float = live_tiles.astype(jnp.float32)
    row_place = (tile_row[:, None] == jnp.arange(blocks)[None, :]).astype(jnp.float32) * live_float[
        :, None
    ]
    picked = jnp.take(sources, tile_col, axis=1)
    products = jnp.einsum("otb,tab->ota", picked, adj_tiles, preferred_element_type=jnp.float32)
    summed = jnp.einsum(
        "ota,tr->ora", products, row_place, precision=lax.Precision.HIGHEST
    ).reshape(feat_rows, node_rows)
    preact = summed + bias_vec.astype(jnp.float32)[:, None]
    activated, pullback = jax.vjp(smooth_gate, preact)
    grad_pre = pullback(cotangent.astype(jnp.float32))[0]
    grad_low = grad_pre.astype(jnp.bfloat16)
    grad_blocks = grad_low.reshape(feat_rows, blocks, tile_size)
    rows_picked = jnp.take(grad_blocks, tile_row, axis=1)
    backward = jnp.einsum(
        "ota,tab->otb", rows_picked, adj_tiles, preferred_element_type=jnp.float32
    )
    src_place = (tile_col[:, None] == jnp.arange(blocks)[None, :]).astype(
        jnp.float32
    ) * live_float[:, None]
    recv_place = (send_block[:, None] == jnp.arange(blocks)[None, :]).astype(jnp.float32)
    own_sum = jnp.einsum(
        "otb,tr->orb", backward, src_place, precision=lax.Precision.HIGHEST
    )
    slot_hit = jnp.logical_and(
        tile_col[:, None] == blocks + jnp.arange(domains)[None, :], live_tiles[:, None]
    )
    hit_tile = jnp.sum(jnp.where(slot_hit, jnp.arange(tile_slots)[:, None], 0), axis=0)
    has_hit = jnp.any(slot_hit, axis=0)
    out_parts = jnp.where(
        has_hit[None, :, None], jnp.take(backward, hit_tile, axis=1), 0.0
    )
    in_parts = lax.all_to_all(out_parts, "dom", split_axis=1, concat_axis=1, tiled=True)
    grad_sum = own_sum + jnp.einsum(
        "oqb,qr->orb", in_parts, recv_place, precision=lax.Precision.HIGHEST
    )
    grad_hidden = grad_sum.reshape(feat_rows, node_rows).astype(jnp.bfloat16)
    norm_scale = 1.0 / math.sqrt(domains * node_rows)
    weight_part = lax.dot_general(
        whole, grad_hidden, (((1,), (1,)), ((), ())), preferred_element_type=jnp.float32
    )
    bias_part = jnp.sum(grad_pre, axis=1)
    packed = jnp.concatenate([weight_part, bias_part[None, :]], axis=0)
    packed = scatter_gather_sum(packed, "dom", domains)
    grad_weight = packed[:-1] * norm_scale
    grad_bias = packed[-1] * norm_scale
    full_weight = jnp.concatenate(list(group_stack(weight, "feat", parts, 1, parts)), axis=1)
    all_grad = group_stack(grad_hidden, "feat", parts, 1, parts).reshape(parts * feat_rows, node_rows)
    my_rows = lax.dynamic_slice_in_dim(
        full_weight, lax.axis_index("feat") * feat_rows, feat_rows, 0
    )
    grad_input = jnp.dot(my_rows, all_grad, preferred_element_type=jnp.float32).astype(jnp.bfloat16)
    return (activated.astype(jnp.bfloat16), grad_input, grad_weight, grad_bias)


def solution(mesh):
    placed = (
        P("feat", "dom"),
        P(None, "feat"),
        P("feat"),
        P("dom", None, None),
        P("dom"),
        P("dom"),
        P("dom"),
        P("dom"),
        P("feat", "dom"),
    )
    return jax.shard_map(
        per_device,
        mesh=mesh,
        in_specs=placed,
        out_specs=(P("feat", "dom"), P("feat", "dom"), P(None, "feat"), P("feat")),
        check_vma=False,
    )
```

```python
import math

import jax
import jax.numpy as jnp
from jax import lax
from jax.sharding import PartitionSpec as P


def smooth_gate(values):
    return jax.nn.gelu(values, approximate=True)


def group_stack(values, axis, size, stride, count):
    received = [values]
    for offset in range(1, count):
        pairs = [(i, i ^ (offset * stride)) for i in range(size)]
        received.append(lax.ppermute(values, axis, pairs))
    stacked = jnp.stack(received)
    mine = (lax.axis_index(axis) // stride) % count
    return jnp.take(stacked, mine ^ jnp.arange(count), axis=0)


def scatter_gather_sum(values, axis, size):
    rows, cols = values.shape
    chunk = -(-rows // size)
    padded = jnp.pad(values, ((0, chunk * size - rows), (0, 0))).reshape(size, chunk, cols)
    gathered = lax.all_to_all(padded, axis, 0, 0, tiled=True)
    reduced = jnp.sum(gathered, axis=0)
    spread = jnp.broadcast_to(reduced[None], (size, chunk, cols))
    total = lax.all_to_all(spread, axis, 0, 0, tiled=True)
    return total.reshape(size * chunk, cols)[:rows]


def per_device(
    node_feats, weight, bias_vec, adj_tiles, tile_row, tile_col, tile_count, send_block, cotangent
):
    feat_rows, node_rows = node_feats.shape
    tile_slots = adj_tiles.shape[0]
    tile_size = adj_tiles.shape[1]
    blocks = node_rows // tile_size
    domains = lax.axis_size("dom")
    parts = lax.axis_size("feat")
    live_tiles = jnp.arange(tile_slots) < tile_count[0]
    slot_hit = jnp.logical_and(
        tile_col[:, None] == blocks + jnp.arange(domains)[None, :], live_tiles[:, None]
    )
    hit_tile = jnp.sum(jnp.where(slot_hit, jnp.arange(tile_slots)[:, None], 0), axis=0)
    has_hit = jnp.any(slot_hit, axis=0)
    slot_rows = jnp.sum(jnp.where(slot_hit, tile_row[:, None], 0), axis=0)
    quarter = tile_size // parts
    my_quarter = lax.dynamic_slice_in_dim(
        adj_tiles, lax.axis_index("feat") * quarter, quarter, 1
    )
    out_quarters = jnp.where(
        has_hit[:, None, None], jnp.take(my_quarter, hit_tile, axis=0), jnp.zeros((), adj_tiles.dtype)
    )
    in_quarters = lax.all_to_all(out_quarters, "dom", split_axis=0, concat_axis=0, tiled=True)
    in_tiles = jnp.moveaxis(group_stack(in_quarters, "feat", parts, 1, parts), 0, 1).reshape(
        domains, tile_size, tile_size
    )

    def in_rows(grad_blocks):
        out_rows = jnp.take(grad_blocks, slot_rows, axis=1)
        return lax.all_to_all(out_rows, "dom", split_axis=1, concat_axis=1, tiled=True)

    whole = group_stack(node_feats, "feat", parts, 1, parts).reshape(parts * feat_rows, node_rows)
    hidden = lax.dot_general(
        weight, whole, (((0,), (0,)), ((), ())), preferred_element_type=jnp.float32
    ).astype(jnp.bfloat16)
    hid_blocks = hidden.reshape(feat_rows, blocks, tile_size)
    outgoing = jnp.take(hid_blocks, send_block, axis=1)
    incoming = lax.all_to_all(outgoing, "dom", split_axis=1, concat_axis=1, tiled=True)
    sources = jnp.concatenate([hid_blocks, incoming], axis=1)
    live_float = live_tiles.astype(jnp.float32)
    row_place = (tile_row[:, None] == jnp.arange(blocks)[None, :]).astype(jnp.float32) * live_float[
        :, None
    ]
    picked = jnp.take(sources, tile_col, axis=1)
    products = jnp.einsum("otb,tab->ota", picked, adj_tiles, preferred_element_type=jnp.float32)
    summed = jnp.einsum(
        "ota,tr->ora", products, row_place, precision=lax.Precision.HIGHEST
    ).reshape(feat_rows, node_rows)
    preact = summed + bias_vec.astype(jnp.float32)[:, None]
    activated, pullback = jax.vjp(smooth_gate, preact)
    grad_pre = pullback(cotangent.astype(jnp.float32))[0]
    grad_low = grad_pre.astype(jnp.bfloat16)
    grad_blocks = grad_low.reshape(feat_rows, blocks, tile_size)
    rows_picked = jnp.take(grad_blocks, tile_row, axis=1)
    backward = jnp.einsum(
        "ota,tab->otb", rows_picked, adj_tiles, preferred_element_type=jnp.float32
    )
    src_place = (tile_col[:, None] == jnp.arange(blocks)[None, :]).astype(
        jnp.float32
    ) * live_float[:, None]
    recv_place = (send_block[:, None] == jnp.arange(blocks)[None, :]).astype(jnp.float32)
    own_sum = jnp.einsum(
        "otb,tr->orb", backward, src_place, precision=lax.Precision.HIGHEST
    )
    remote_sum = jnp.einsum("opa,pab->opb", in_rows(grad_blocks), in_tiles, preferred_element_type=jnp.float32)
    grad_sum = own_sum + jnp.einsum(
        "oqb,qr->orb", remote_sum, recv_place, precision=lax.Precision.HIGHEST
    )
    grad_hidden = grad_sum.reshape(feat_rows, node_rows).astype(jnp.bfloat16)
    norm_scale = 1.0 / math.sqrt(domains * node_rows)
    weight_part = lax.dot_general(
        whole, grad_hidden, (((1,), (1,)), ((), ())), preferred_element_type=jnp.float32
    )
    bias_part = jnp.sum(grad_pre, axis=1)
    packed = jnp.concatenate([weight_part, bias_part[None, :]], axis=0)
    packed = scatter_gather_sum(packed, "dom", domains)
    grad_weight = packed[:-1] * norm_scale
    grad_bias = packed[-1] * norm_scale
    full_weight = jnp.concatenate(list(group_stack(weight, "feat", parts, 1, parts)), axis=1)
    all_grad = group_stack(grad_hidden, "feat", parts, 1, parts).reshape(parts * feat_rows, node_rows)
    my_rows = lax.dynamic_slice_in_dim(
        full_weight, lax.axis_index("feat") * feat_rows, feat_rows, 0
    )
    grad_input = jnp.dot(my_rows, all_grad, preferred_element_type=jnp.float32).astype(jnp.bfloat16)
    return (activated.astype(jnp.bfloat16), grad_input, grad_weight, grad_bias)


def solution(mesh):
    placed = (
        P("feat", "dom"),
        P(None, "feat"),
        P("feat"),
        P("dom", None, None),
        P("dom"),
        P("dom"),
        P("dom"),
        P("dom"),
        P("feat", "dom"),
    )
    return jax.shard_map(
        per_device,
        mesh=mesh,
        in_specs=placed,
        out_specs=(P("feat", "dom"), P("feat", "dom"), P(None, "feat"), P("feat")),
        check_vma=False,
    )
```

```python
import math

import jax
import jax.numpy as jnp
from jax import lax
from jax.sharding import PartitionSpec as P


def smooth_gate(values):
    return jax.nn.gelu(values, approximate=True)


def group_stack(values, axis, size, stride, count):
    received = [values]
    for offset in range(1, count):
        pairs = [(i, i ^ (offset * stride)) for i in range(size)]
        received.append(lax.ppermute(values, axis, pairs))
    stacked = jnp.stack(received)
    mine = (lax.axis_index(axis) // stride) % count
    return jnp.take(stacked, mine ^ jnp.arange(count), axis=0)


def scatter_gather_sum(values, axis, size):
    rows, cols = values.shape
    chunk = -(-rows // size)
    padded = jnp.pad(values, ((0, chunk * size - rows), (0, 0))).reshape(size, chunk, cols)
    gathered = lax.all_to_all(padded, axis, 0, 0, tiled=True)
    reduced = jnp.sum(gathered, axis=0)
    spread = jnp.broadcast_to(reduced[None], (size, chunk, cols))
    total = lax.all_to_all(spread, axis, 0, 0, tiled=True)
    return total.reshape(size * chunk, cols)[:rows]


def per_device(
    node_feats, weight, bias_vec, adj_tiles, tile_row, tile_col, tile_count, send_block, cotangent
):
    feat_rows, node_rows = node_feats.shape
    tile_slots = adj_tiles.shape[0]
    tile_size = adj_tiles.shape[1]
    blocks = node_rows // tile_size
    domains = lax.axis_size("dom")
    parts = lax.axis_size("feat")
    live_tiles = jnp.arange(tile_slots) < tile_count[0]
    slot_hit = jnp.logical_and(
        tile_col[:, None] == blocks + jnp.arange(domains)[None, :], live_tiles[:, None]
    )
    hit_tile = jnp.sum(jnp.where(slot_hit, jnp.arange(tile_slots)[:, None], 0), axis=0)
    has_hit = jnp.any(slot_hit, axis=0)
    slot_rows = jnp.sum(jnp.where(slot_hit, tile_row[:, None], 0), axis=0)
    quarter = tile_size // parts
    my_quarter = lax.dynamic_slice_in_dim(
        adj_tiles, lax.axis_index("feat") * quarter, quarter, 1
    )
    out_quarters = jnp.where(
        has_hit[:, None, None], jnp.take(my_quarter, hit_tile, axis=0), jnp.zeros((), adj_tiles.dtype)
    )
    in_quarters = lax.all_to_all(out_quarters, "dom", split_axis=0, concat_axis=0, tiled=True)

    def in_rows(grad_blocks):
        out_rows = jnp.take(grad_blocks, slot_rows, axis=1)
        return lax.all_to_all(out_rows, "dom", split_axis=1, concat_axis=1, tiled=True)

    whole = group_stack(node_feats, "feat", parts, 1, parts).reshape(parts * feat_rows, node_rows)
    hidden = lax.dot_general(
        weight, whole, (((0,), (0,)), ((), ())), preferred_element_type=jnp.float32
    ).astype(jnp.bfloat16)
    hid_blocks = hidden.reshape(feat_rows, blocks, tile_size)
    outgoing = jnp.take(hid_blocks, send_block, axis=1)
    outgoing, in_quarters = lax.optimization_barrier((outgoing, in_quarters))
    in_tiles = jnp.moveaxis(group_stack(in_quarters, "feat", parts, 1, parts), 0, 1).reshape(
        domains, tile_size, tile_size
    )
    incoming = lax.all_to_all(outgoing, "dom", split_axis=1, concat_axis=1, tiled=True)
    incoming, in_tiles = lax.optimization_barrier((incoming, in_tiles))
    sources = jnp.concatenate([hid_blocks, incoming], axis=1)
    live_float = live_tiles.astype(jnp.float32)
    row_place = (tile_row[:, None] == jnp.arange(blocks)[None, :]).astype(jnp.float32) * live_float[
        :, None
    ]
    picked = jnp.take(sources, tile_col, axis=1)
    products = jnp.einsum("otb,tab->ota", picked, adj_tiles, preferred_element_type=jnp.float32)
    summed = jnp.einsum(
        "ota,tr->ora", products, row_place, precision=lax.Precision.HIGHEST
    ).reshape(feat_rows, node_rows)
    preact = summed + bias_vec.astype(jnp.float32)[:, None]
    activated, pullback = jax.vjp(smooth_gate, preact)
    grad_pre = pullback(cotangent.astype(jnp.float32))[0]
    grad_low = grad_pre.astype(jnp.bfloat16)
    grad_blocks = grad_low.reshape(feat_rows, blocks, tile_size)
    rows_picked = jnp.take(grad_blocks, tile_row, axis=1)
    backward = jnp.einsum(
        "ota,tab->otb", rows_picked, adj_tiles, preferred_element_type=jnp.float32
    )
    src_place = (tile_col[:, None] == jnp.arange(blocks)[None, :]).astype(
        jnp.float32
    ) * live_float[:, None]
    recv_place = (send_block[:, None] == jnp.arange(blocks)[None, :]).astype(jnp.float32)
    own_sum = jnp.einsum(
        "otb,tr->orb", backward, src_place, precision=lax.Precision.HIGHEST
    )
    remote_sum = jnp.einsum("opa,pab->opb", in_rows(grad_blocks), in_tiles, preferred_element_type=jnp.float32)
    grad_sum = own_sum + jnp.einsum(
        "oqb,qr->orb", remote_sum, recv_place, precision=lax.Precision.HIGHEST
    )
    grad_hidden = grad_sum.reshape(feat_rows, node_rows).astype(jnp.bfloat16)
    norm_scale = 1.0 / math.sqrt(domains * node_rows)
    weight_part = lax.dot_general(
        whole, grad_hidden, (((1,), (1,)), ((), ())), preferred_element_type=jnp.float32
    )
    bias_part = jnp.sum(grad_pre, axis=1)
    packed = jnp.concatenate([weight_part, bias_part[None, :]], axis=0)
    packed = scatter_gather_sum(packed, "dom", domains)
    grad_weight = packed[:-1] * norm_scale
    grad_bias = packed[-1] * norm_scale
    full_weight = jnp.concatenate(list(group_stack(weight, "feat", parts, 1, parts)), axis=1)
    all_grad = group_stack(grad_hidden, "feat", parts, 1, parts).reshape(parts * feat_rows, node_rows)
    my_rows = lax.dynamic_slice_in_dim(
        full_weight, lax.axis_index("feat") * feat_rows, feat_rows, 0
    )
    grad_input = jnp.dot(my_rows, all_grad, preferred_element_type=jnp.float32).astype(jnp.bfloat16)
    return (activated.astype(jnp.bfloat16), grad_input, grad_weight, grad_bias)


def solution(mesh):
    placed = (
        P("feat", "dom"),
        P(None, "feat"),
        P("feat"),
        P("dom", None, None),
        P("dom"),
        P("dom"),
        P("dom"),
        P("dom"),
        P("feat", "dom"),
    )
    return jax.shard_map(
        per_device,
        mesh=mesh,
        in_specs=placed,
        out_specs=(P("feat", "dom"), P("feat", "dom"), P(None, "feat"), P("feat")),
        check_vma=False,
    )
```

```python
import math

import jax
import jax.numpy as jnp
from jax import lax
from jax.sharding import PartitionSpec as P


def smooth_gate(values):
    return jax.nn.gelu(values, approximate=True)


def group_stack(values, axis, size, stride, count):
    received = [values]
    for offset in range(1, count):
        pairs = [(i, i ^ (offset * stride)) for i in range(size)]
        received.append(lax.ppermute(values, axis, pairs))
    stacked = jnp.stack(received)
    mine = (lax.axis_index(axis) // stride) % count
    return jnp.take(stacked, mine ^ jnp.arange(count), axis=0)


def scatter_gather_sum(values, axis, size):
    rows, cols = values.shape
    chunk = -(-rows // size)
    padded = jnp.pad(values, ((0, chunk * size - rows), (0, 0))).reshape(size, chunk, cols)
    gathered = lax.all_to_all(padded, axis, 0, 0, tiled=True)
    reduced = jnp.sum(gathered, axis=0)
    spread = jnp.broadcast_to(reduced[None], (size, chunk, cols))
    total = lax.all_to_all(spread, axis, 0, 0, tiled=True)
    return total.reshape(size * chunk, cols)[:rows]


def per_device(
    node_feats, weight, bias_vec, adj_tiles, tile_row, tile_col, tile_count, send_block, cotangent
):
    feat_rows, node_rows = node_feats.shape
    tile_slots = adj_tiles.shape[0]
    tile_size = adj_tiles.shape[1]
    blocks = node_rows // tile_size
    domains = lax.axis_size("dom")
    parts = lax.axis_size("feat")
    whole = group_stack(node_feats, "feat", parts, 1, parts).reshape(parts * feat_rows, node_rows)
    hidden = lax.dot_general(
        weight, whole, (((0,), (0,)), ((), ())), preferred_element_type=jnp.float32
    ).astype(jnp.bfloat16)
    hid_blocks = hidden.reshape(feat_rows, blocks, tile_size)
    outgoing = jnp.take(hid_blocks, send_block, axis=1)
    incoming = lax.all_to_all(outgoing, "dom", split_axis=1, concat_axis=1, tiled=True)
    sources = jnp.concatenate([hid_blocks, incoming], axis=1)
    live_tiles = jnp.arange(tile_slots) < tile_count[0]
    live_float = live_tiles.astype(jnp.float32)
    row_place = (tile_row[:, None] == jnp.arange(blocks)[None, :]).astype(jnp.float32) * live_float[
        :, None
    ]
    picked = jnp.take(sources, tile_col, axis=1)
    products = jnp.einsum("otb,tab->ota", picked, adj_tiles, preferred_element_type=jnp.float32)
    summed = jnp.einsum(
        "ota,tr->ora", products, row_place, precision=lax.Precision.HIGHEST
    ).reshape(feat_rows, node_rows)
    preact = summed + bias_vec.astype(jnp.float32)[:, None]
    activated, pullback = jax.vjp(smooth_gate, preact)
    grad_pre = pullback(cotangent.astype(jnp.float32))[0]
    grad_low = grad_pre.astype(jnp.bfloat16)
    grad_blocks = grad_low.reshape(feat_rows, blocks, tile_size)
    rows_picked = jnp.take(grad_blocks, tile_row, axis=1)
    backward = jnp.einsum(
        "ota,tab->otb", rows_picked, adj_tiles, preferred_element_type=jnp.float32
    )
    src_place = (tile_col[:, None] == jnp.arange(blocks)[None, :]).astype(
        jnp.float32
    ) * live_float[:, None]
    recv_place = (send_block[:, None] == jnp.arange(blocks)[None, :]).astype(jnp.float32)
    own_sum = jnp.einsum(
        "otb,tr->orb", backward, src_place, precision=lax.Precision.HIGHEST
    )
    slot_hit = jnp.logical_and(
        tile_col[:, None] == blocks + jnp.arange(domains)[None, :], live_tiles[:, None]
    )
    hit_tile = jnp.sum(jnp.where(slot_hit, jnp.arange(tile_slots)[:, None], 0), axis=0)
    has_hit = jnp.any(slot_hit, axis=0)
    out_parts = jnp.where(
        has_hit[None, :, None], jnp.take(backward, hit_tile, axis=1), 0.0
    ).astype(jnp.bfloat16)
    in_parts = lax.all_to_all(out_parts, "dom", split_axis=1, concat_axis=1, tiled=True)
    remote_sum = in_parts.astype(jnp.float32)
    grad_sum = own_sum + jnp.einsum(
        "oqb,qr->orb", remote_sum, recv_place, precision=lax.Precision.HIGHEST
    )
    grad_hidden = grad_sum.reshape(feat_rows, node_rows).astype(jnp.bfloat16)
    norm_scale = 1.0 / math.sqrt(domains * node_rows)
    weight_part = lax.dot_general(
        whole, grad_hidden, (((1,), (1,)), ((), ())), preferred_element_type=jnp.float32
    )
    bias_part = jnp.sum(grad_pre, axis=1)
    packed = jnp.concatenate([weight_part, bias_part[None, :]], axis=0)
    packed = scatter_gather_sum(packed, "dom", domains)
    grad_weight = packed[:-1] * norm_scale
    grad_bias = packed[-1] * norm_scale
    full_weight = jnp.concatenate(list(group_stack(weight, "feat", parts, 1, parts)), axis=1)
    all_grad = group_stack(grad_hidden, "feat", parts, 1, parts).reshape(parts * feat_rows, node_rows)
    my_rows = lax.dynamic_slice_in_dim(
        full_weight, lax.axis_index("feat") * feat_rows, feat_rows, 0
    )
    grad_input = jnp.dot(my_rows, all_grad, preferred_element_type=jnp.float32).astype(jnp.bfloat16)
    return (activated.astype(jnp.bfloat16), grad_input, grad_weight, grad_bias)


def solution(mesh):
    placed = (
        P("feat", "dom"),
        P(None, "feat"),
        P("feat"),
        P("dom", None, None),
        P("dom"),
        P("dom"),
        P("dom"),
        P("dom"),
        P("feat", "dom"),
    )
    return jax.shard_map(
        per_device,
        mesh=mesh,
        in_specs=placed,
        out_specs=(P("feat", "dom"), P("feat", "dom"), P(None, "feat"), P("feat")),
        check_vma=False,
    )
```

```python
import math

import jax
import jax.numpy as jnp
from jax import lax
from jax.sharding import PartitionSpec as P


def smooth_gate(values):
    return jax.nn.gelu(values, approximate=True)


def group_stack(values, axis, size, stride, count):
    received = [values]
    for offset in range(1, count):
        pairs = [(i, i ^ (offset * stride)) for i in range(size)]
        received.append(lax.ppermute(values, axis, pairs))
    stacked = jnp.stack(received)
    mine = (lax.axis_index(axis) // stride) % count
    return jnp.take(stacked, mine ^ jnp.arange(count), axis=0, mode="clip")


def exchange_order(values, axis, size, count, dim=0):
    received = [values]
    for offset in range(1, count):
        pairs = [(i, i ^ offset) for i in range(size)]
        received.append(lax.ppermute(values, axis, pairs))
    return jnp.concatenate(received, axis=dim)


def scatter_gather_sum(values, axis, size):
    rows, cols = values.shape
    chunk = -(-rows // size)
    padded = jnp.pad(values, ((0, chunk * size - rows), (0, 0))).reshape(size, chunk, cols)
    gathered = lax.all_to_all(padded, axis, 0, 0, tiled=True)
    reduced = jnp.sum(gathered, axis=0)
    spread = jnp.broadcast_to(reduced[None], (size, chunk, cols))
    total = lax.all_to_all(spread, axis, 0, 0, tiled=True)
    return total.reshape(size * chunk, cols)[:rows]


def per_device(
    node_feats, weight, bias_vec, adj_tiles, tile_row, tile_col, tile_count, send_block, cotangent
):
    feat_rows, node_rows = node_feats.shape
    tile_slots = adj_tiles.shape[0]
    tile_size = adj_tiles.shape[1]
    blocks = node_rows // tile_size
    domains = lax.axis_size("dom")
    parts = lax.axis_size("feat")
    live_tiles = jnp.arange(tile_slots) < tile_count[0]
    slot_hit = jnp.logical_and(
        tile_col[:, None] == blocks + jnp.arange(domains)[None, :], live_tiles[:, None]
    )
    hit_tile = jnp.sum(jnp.where(slot_hit, jnp.arange(tile_slots)[:, None], 0), axis=0)
    has_hit = jnp.any(slot_hit, axis=0)
    slot_rows = jnp.sum(jnp.where(slot_hit, tile_row[:, None], 0), axis=0)
    peer_tiles = jnp.where(
        has_hit[:, None, None],
        jnp.take(adj_tiles, hit_tile, axis=0, mode="clip"),
        jnp.zeros((), adj_tiles.dtype),
    )
    order = lax.axis_index("feat") ^ jnp.arange(parts)
    whole = exchange_order(node_feats, "feat", parts, parts)
    in_rows = weight.shape[0] // parts
    weight_ordered = jnp.take(
        weight.reshape(parts, in_rows, weight.shape[1]), order, axis=0, mode="clip"
    ).reshape(weight.shape)
    hidden = lax.dot_general(
        weight_ordered, whole, (((0,), (0,)), ((), ())), preferred_element_type=jnp.float32
    ).astype(jnp.bfloat16)
    hid_blocks = hidden.reshape(feat_rows, blocks, tile_size)
    outgoing = jnp.take(hid_blocks, send_block, axis=1, mode="clip")
    incoming = lax.all_to_all(outgoing, "dom", split_axis=1, concat_axis=1, tiled=True)
    sources = jnp.concatenate([hid_blocks, incoming], axis=1)
    live_float = live_tiles.astype(jnp.float32)
    row_place = (tile_row[:, None] == jnp.arange(blocks)[None, :]).astype(jnp.float32) * live_float[
        :, None
    ]
    picked = jnp.take(sources, tile_col, axis=1, mode="clip")
    products = jnp.einsum("otb,tab->ota", picked, adj_tiles, preferred_element_type=jnp.float32)
    summed = jnp.einsum(
        "ota,tr->ora", products, row_place, precision=lax.Precision.HIGHEST
    ).reshape(feat_rows, node_rows)
    preact = summed + bias_vec.astype(jnp.float32)[:, None]
    activated, pullback = jax.vjp(smooth_gate, preact)
    grad_pre = pullback(cotangent.astype(jnp.float32))[0]
    grad_low = grad_pre.astype(jnp.bfloat16)
    grad_blocks = grad_low.reshape(feat_rows, blocks, tile_size)
    rows_picked = jnp.take(grad_blocks, tile_row, axis=1, mode="clip")
    backward = jnp.einsum(
        "ota,tab->otb", rows_picked, adj_tiles, preferred_element_type=jnp.float32
    )
    src_place = (tile_col[:, None] == jnp.arange(blocks)[None, :]).astype(
        jnp.float32
    ) * live_float[:, None]
    recv_place = (send_block[:, None] == jnp.arange(blocks)[None, :]).astype(jnp.float32)
    own_sum = jnp.einsum(
        "otb,tr->orb", backward, src_place, precision=lax.Precision.HIGHEST
    )
    out_rows = jnp.take(grad_blocks, slot_rows, axis=1, mode="clip")
    out_parts = jnp.einsum(
        "oqa,qab->oqb", out_rows, peer_tiles, preferred_element_type=jnp.float32
    ).astype(jnp.bfloat16)
    in_parts = lax.all_to_all(out_parts, "dom", split_axis=1, concat_axis=1, tiled=True)
    remote_sum = in_parts.astype(jnp.float32)
    grad_sum = own_sum + jnp.einsum(
        "oqb,qr->orb", remote_sum, recv_place, precision=lax.Precision.HIGHEST
    )
    grad_hidden = grad_sum.reshape(feat_rows, node_rows).astype(jnp.bfloat16)
    norm_scale = 1.0 / math.sqrt(domains * node_rows)
    weight_part = lax.dot_general(
        whole, grad_hidden, (((1,), (1,)), ((), ())), preferred_element_type=jnp.float32
    )
    weight_part = jnp.take(
        weight_part.reshape(parts, in_rows, feat_rows), order, axis=0, mode="clip"
    ).reshape(weight_part.shape)
    bias_part = jnp.sum(grad_pre, axis=1)
    packed = jnp.concatenate([weight_part, bias_part[None, :]], axis=0)
    packed = scatter_gather_sum(packed, "dom", domains)
    grad_weight = packed[:-1] * norm_scale
    grad_bias = packed[-1] * norm_scale
    full_weight = exchange_order(weight, "feat", parts, parts, dim=1)
    all_grad = exchange_order(grad_hidden, "feat", parts, parts)
    my_rows = lax.dynamic_slice_in_dim(
        full_weight, lax.axis_index("feat") * feat_rows, feat_rows, 0
    )
    grad_input = jnp.dot(my_rows, all_grad, preferred_element_type=jnp.float32).astype(jnp.bfloat16)
    return (activated.astype(jnp.bfloat16), grad_input, grad_weight, grad_bias)


def solution(mesh):
    placed = (
        P("feat", "dom"),
        P(None, "feat"),
        P("feat"),
        P("dom", None, None),
        P("dom"),
        P("dom"),
        P("dom"),
        P("dom"),
        P("feat", "dom"),
    )
    return jax.shard_map(
        per_device,
        mesh=mesh,
        in_specs=placed,
        out_specs=(P("feat", "dom"), P("feat", "dom"), P(None, "feat"), P("feat")),
        check_vma=False,
    )
```

```python
import math

import jax
import jax.numpy as jnp
from jax import lax
from jax.sharding import PartitionSpec as P


def smooth_gate(values):
    return jax.nn.gelu(values, approximate=True)


def group_stack(values, axis, size, stride, count):
    received = [values]
    for offset in range(1, count):
        pairs = [(i, i ^ (offset * stride)) for i in range(size)]
        received.append(lax.ppermute(values, axis, pairs))
    stacked = jnp.stack(received)
    mine = (lax.axis_index(axis) // stride) % count
    return jnp.take(stacked, mine ^ jnp.arange(count), axis=0, mode="clip")


def exchange_order(values, axis, size, count, dim=0):
    received = [values]
    for offset in range(1, count):
        pairs = [(i, i ^ offset) for i in range(size)]
        received.append(lax.ppermute(values, axis, pairs))
    return received


def scatter_gather_sum(values, axis, size):
    rows, cols = values.shape
    chunk = -(-rows // size)
    padded = jnp.pad(values, ((0, chunk * size - rows), (0, 0))).reshape(size, chunk, cols)
    gathered = lax.all_to_all(padded, axis, 0, 0, tiled=True)
    reduced = jnp.sum(gathered, axis=0)
    spread = jnp.broadcast_to(reduced[None], (size, chunk, cols))
    total = lax.all_to_all(spread, axis, 0, 0, tiled=True)
    return total.reshape(size * chunk, cols)[:rows]


def per_device(
    node_feats, weight, bias_vec, adj_tiles, tile_row, tile_col, tile_count, send_block, cotangent
):
    feat_rows, node_rows = node_feats.shape
    tile_slots = adj_tiles.shape[0]
    tile_size = adj_tiles.shape[1]
    blocks = node_rows // tile_size
    domains = lax.axis_size("dom")
    parts = lax.axis_size("feat")
    live_tiles = jnp.arange(tile_slots) < tile_count[0]
    slot_hit = jnp.logical_and(
        tile_col[:, None] == blocks + jnp.arange(domains)[None, :], live_tiles[:, None]
    )
    hit_tile = jnp.sum(jnp.where(slot_hit, jnp.arange(tile_slots)[:, None], 0), axis=0)
    has_hit = jnp.any(slot_hit, axis=0)
    slot_rows = jnp.sum(jnp.where(slot_hit, tile_row[:, None], 0), axis=0)
    peer_tiles = jnp.where(
        has_hit[:, None, None],
        jnp.take(adj_tiles, hit_tile, axis=0, mode="clip"),
        jnp.zeros((), adj_tiles.dtype),
    )
    order = lax.axis_index("feat") ^ jnp.arange(parts)
    pieces = exchange_order(node_feats, "feat", parts, parts)
    in_rows = weight.shape[0] // parts
    weight_ordered = jnp.take(
        weight.reshape(parts, in_rows, weight.shape[1]), order, axis=0, mode="clip"
    )
    hidden = sum(
        lax.dot_general(
            weight_ordered[s], piece, (((0,), (0,)), ((), ())), preferred_element_type=jnp.float32
        )
        for s, piece in enumerate(pieces)
    ).astype(jnp.bfloat16)
    hid_blocks = hidden.reshape(feat_rows, blocks, tile_size)
    outgoing = jnp.take(hid_blocks, send_block, axis=1, mode="clip")
    incoming = lax.all_to_all(outgoing, "dom", split_axis=1, concat_axis=1, tiled=True)
    live_float = live_tiles.astype(jnp.float32)
    local_ok = jnp.logical_and(live_tiles, tile_col < blocks).astype(jnp.float32)
    row_place = (tile_row[:, None] == jnp.arange(blocks)[None, :]).astype(jnp.float32) * local_ok[
        :, None
    ]
    picked = jnp.take(hid_blocks, jnp.minimum(tile_col, blocks - 1), axis=1, mode="clip")
    products = jnp.einsum("otb,tab->ota", picked, adj_tiles, preferred_element_type=jnp.float32)
    summed_local = jnp.einsum("ota,tr->ora", products, row_place, precision=lax.Precision.HIGHEST)
    summed_local, incoming = lax.optimization_barrier((summed_local, incoming))
    far_place = (slot_rows[:, None] == jnp.arange(blocks)[None, :]).astype(jnp.float32) * has_hit[
        :, None
    ].astype(jnp.float32)
    far_products = jnp.einsum(
        "oqb,qab->oqa", incoming, peer_tiles, preferred_element_type=jnp.float32
    )
    summed_far = jnp.einsum("oqa,qr->ora", far_products, far_place, precision=lax.Precision.HIGHEST)
    summed = (summed_local + summed_far).reshape(feat_rows, node_rows)
    preact = summed + bias_vec.astype(jnp.float32)[:, None]
    activated, pullback = jax.vjp(smooth_gate, preact)
    grad_pre = pullback(cotangent.astype(jnp.float32))[0]
    grad_low = grad_pre.astype(jnp.bfloat16)
    grad_blocks = grad_low.reshape(feat_rows, blocks, tile_size)
    rows_picked = jnp.take(grad_blocks, tile_row, axis=1, mode="clip")
    backward = jnp.einsum(
        "ota,tab->otb", rows_picked, adj_tiles, preferred_element_type=jnp.float32
    )
    src_place = (tile_col[:, None] == jnp.arange(blocks)[None, :]).astype(
        jnp.float32
    ) * live_float[:, None]
    recv_place = (send_block[:, None] == jnp.arange(blocks)[None, :]).astype(jnp.float32)
    own_sum = jnp.einsum(
        "otb,tr->orb", backward, src_place, precision=lax.Precision.HIGHEST
    )
    out_rows = jnp.take(grad_blocks, slot_rows, axis=1, mode="clip")
    out_parts = jnp.einsum(
        "oqa,qab->oqb", out_rows, peer_tiles, preferred_element_type=jnp.float32
    ).astype(jnp.bfloat16)
    in_parts = lax.all_to_all(out_parts, "dom", split_axis=1, concat_axis=1, tiled=True)
    remote_sum = in_parts.astype(jnp.float32)
    grad_sum = own_sum + jnp.einsum(
        "oqb,qr->orb", remote_sum, recv_place, precision=lax.Precision.HIGHEST
    )
    grad_hidden = grad_sum.reshape(feat_rows, node_rows).astype(jnp.bfloat16)
    norm_scale = 1.0 / math.sqrt(domains * node_rows)
    weight_part = jnp.stack(
        [
            lax.dot_general(
                piece, grad_hidden, (((1,), (1,)), ((), ())), preferred_element_type=jnp.float32
            )
            for piece in pieces
        ]
    )
    weight_part = jnp.take(weight_part, order, axis=0, mode="clip").reshape(
        parts * in_rows, feat_rows
    )
    bias_part = jnp.sum(grad_pre, axis=1)
    packed = jnp.concatenate([weight_part, bias_part[None, :]], axis=0)
    packed = scatter_gather_sum(packed, "dom", domains)
    grad_weight = packed[:-1] * norm_scale
    grad_bias = packed[-1] * norm_scale
    full_weight = jnp.concatenate(exchange_order(weight, "feat", parts, parts), axis=1)
    all_grad = jnp.concatenate(exchange_order(grad_hidden, "feat", parts, parts), axis=0)
    my_rows = lax.dynamic_slice_in_dim(
        full_weight, lax.axis_index("feat") * feat_rows, feat_rows, 0
    )
    grad_input = jnp.dot(my_rows, all_grad, preferred_element_type=jnp.float32).astype(jnp.bfloat16)
    return (activated.astype(jnp.bfloat16), grad_input, grad_weight, grad_bias)


def solution(mesh):
    placed = (
        P("feat", "dom"),
        P(None, "feat"),
        P("feat"),
        P("dom", None, None),
        P("dom"),
        P("dom"),
        P("dom"),
        P("dom"),
        P("feat", "dom"),
    )
    return jax.shard_map(
        per_device,
        mesh=mesh,
        in_specs=placed,
        out_specs=(P("feat", "dom"), P("feat", "dom"), P(None, "feat"), P("feat")),
        check_vma=False,
    )
```

```python
import math

import jax
import jax.numpy as jnp
from jax import lax
from jax.sharding import PartitionSpec as P


def smooth_gate(values):
    return jax.nn.gelu(values, approximate=True)


def group_stack(values, axis, size, stride, count):
    received = [values]
    for offset in range(1, count):
        pairs = [(i, i ^ (offset * stride)) for i in range(size)]
        received.append(lax.ppermute(values, axis, pairs))
    stacked = jnp.stack(received)
    mine = (lax.axis_index(axis) // stride) % count
    return jnp.take(stacked, mine ^ jnp.arange(count), axis=0, mode="clip")


def exchange_order(values, axis, size, count, dim=0):
    received = [values]
    for offset in range(1, count):
        pairs = [(i, i ^ offset) for i in range(size)]
        received.append(lax.ppermute(values, axis, pairs))
    return received


def scatter_gather_sum(values, axis, size):
    rows, cols = values.shape
    chunk = rows // size
    gathered = lax.all_to_all(values.reshape(size, chunk, cols), axis, 0, 0, tiled=True)
    reduced = jnp.sum(gathered, axis=0)
    spread = jnp.broadcast_to(reduced[None], (size, chunk, cols))
    total = lax.all_to_all(spread, axis, 0, 0, tiled=True)
    return total.reshape(rows, cols)


def per_device(
    node_feats, weight, bias_vec, adj_tiles, tile_row, tile_col, tile_count, send_block, cotangent
):
    feat_rows, node_rows = node_feats.shape
    tile_slots = adj_tiles.shape[0]
    tile_size = adj_tiles.shape[1]
    blocks = node_rows // tile_size
    domains = lax.axis_size("dom")
    parts = lax.axis_size("feat")
    live_tiles = jnp.arange(tile_slots) < tile_count[0]
    slot_hit = jnp.logical_and(
        tile_col[:, None] == blocks + jnp.arange(domains)[None, :], live_tiles[:, None]
    )
    hit_tile = jnp.sum(jnp.where(slot_hit, jnp.arange(tile_slots)[:, None], 0), axis=0)
    has_hit = jnp.any(slot_hit, axis=0)
    slot_rows = jnp.sum(jnp.where(slot_hit, tile_row[:, None], 0), axis=0)
    peer_tiles = jnp.where(
        has_hit[:, None, None],
        jnp.take(adj_tiles, hit_tile, axis=0, mode="clip"),
        jnp.zeros((), adj_tiles.dtype),
    )
    order = lax.axis_index("feat") ^ jnp.arange(parts)
    pieces = exchange_order(node_feats, "feat", parts, parts)
    full_weight = jnp.concatenate(exchange_order(weight, "feat", parts, parts), axis=1)
    pieces, full_weight = lax.optimization_barrier((pieces, full_weight))
    in_rows = weight.shape[0] // parts
    weight_ordered = jnp.take(
        weight.reshape(parts, in_rows, weight.shape[1]), order, axis=0, mode="clip"
    )
    hidden = sum(
        lax.dot_general(
            weight_ordered[s], piece, (((0,), (0,)), ((), ())), preferred_element_type=jnp.float32
        )
        for s, piece in enumerate(pieces)
    ).astype(jnp.bfloat16)
    hid_blocks = hidden.reshape(feat_rows, blocks, tile_size)
    outgoing = jnp.take(hid_blocks, send_block, axis=1, mode="clip")
    incoming = lax.all_to_all(outgoing, "dom", split_axis=1, concat_axis=1, tiled=True)
    live_float = live_tiles.astype(jnp.float32)
    local_ok = jnp.logical_and(live_tiles, tile_col < blocks).astype(jnp.float32)
    row_place = (tile_row[:, None] == jnp.arange(blocks)[None, :]).astype(jnp.float32) * local_ok[
        :, None
    ]
    picked = jnp.take(hid_blocks, jnp.minimum(tile_col, blocks - 1), axis=1, mode="clip")
    products = jnp.einsum("otb,tab->ota", picked, adj_tiles, preferred_element_type=jnp.float32)
    summed_local = jnp.einsum("ota,tr->ora", products, row_place, precision=lax.Precision.HIGHEST)
    summed_local, incoming = lax.optimization_barrier((summed_local, incoming))
    far_place = (slot_rows[:, None] == jnp.arange(blocks)[None, :]).astype(jnp.float32) * has_hit[
        :, None
    ].astype(jnp.float32)
    far_products = jnp.einsum(
        "oqb,qab->oqa", incoming, peer_tiles, preferred_element_type=jnp.float32
    )
    summed_far = jnp.einsum("oqa,qr->ora", far_products, far_place, precision=lax.Precision.HIGHEST)
    summed = (summed_local + summed_far).reshape(feat_rows, node_rows)
    preact = summed + bias_vec.astype(jnp.float32)[:, None]
    activated, pullback = jax.vjp(smooth_gate, preact)
    grad_pre = pullback(cotangent.astype(jnp.float32))[0]
    grad_low = grad_pre.astype(jnp.bfloat16)
    grad_blocks = grad_low.reshape(feat_rows, blocks, tile_size)
    rows_picked = jnp.take(grad_blocks, tile_row, axis=1, mode="clip")
    backward = jnp.einsum(
        "ota,tab->otb", rows_picked, adj_tiles, preferred_element_type=jnp.float32
    )
    src_place = (tile_col[:, None] == jnp.arange(blocks)[None, :]).astype(
        jnp.float32
    ) * live_float[:, None]
    recv_place = (send_block[:, None] == jnp.arange(blocks)[None, :]).astype(jnp.float32)
    own_sum = jnp.einsum(
        "otb,tr->orb", backward, src_place, precision=lax.Precision.HIGHEST
    )
    out_rows = jnp.take(grad_blocks, slot_rows, axis=1, mode="clip")
    out_parts = jnp.einsum(
        "oqa,qab->oqb", out_rows, peer_tiles, preferred_element_type=jnp.float32
    ).astype(jnp.bfloat16)
    in_parts = lax.all_to_all(out_parts, "dom", split_axis=1, concat_axis=1, tiled=True)
    remote_sum = in_parts.astype(jnp.float32)
    grad_sum = own_sum + jnp.einsum(
        "oqb,qr->orb", remote_sum, recv_place, precision=lax.Precision.HIGHEST
    )
    grad_hidden = grad_sum.reshape(feat_rows, node_rows).astype(jnp.bfloat16)
    norm_scale = 1.0 / math.sqrt(domains * node_rows)
    weight_part = jnp.concatenate(
        [
            lax.dot_general(
                grad_hidden, piece, (((1,), (1,)), ((), ())), preferred_element_type=jnp.float32
            )
            for piece in pieces
        ],
        axis=1,
    )
    bias_part = jnp.sum(grad_pre, axis=1)
    lanes = 128
    weight_rows = weight_part.size // lanes
    pack_rows = -(-(weight_rows + 1) // domains) * domains
    packed = jnp.zeros((pack_rows, lanes), jnp.float32)
    packed = packed.at[:weight_rows].set(weight_part.reshape(weight_rows, lanes))
    packed = packed.at[weight_rows, : bias_part.shape[0]].set(bias_part)
    packed = scatter_gather_sum(packed, "dom", domains)
    summed_weight = packed[:weight_rows].reshape(feat_rows, parts, in_rows)
    summed_weight = jnp.take(summed_weight, order, axis=1, mode="clip").reshape(feat_rows, parts * in_rows)
    grad_weight = summed_weight.T * norm_scale
    grad_bias = packed[weight_rows, : bias_part.shape[0]] * norm_scale
    all_grad = jnp.concatenate(exchange_order(grad_hidden, "feat", parts, parts), axis=0)
    my_rows = lax.dynamic_slice_in_dim(
        full_weight, lax.axis_index("feat") * feat_rows, feat_rows, 0
    )
    grad_input = jnp.dot(my_rows, all_grad, preferred_element_type=jnp.float32).astype(jnp.bfloat16)
    return (activated.astype(jnp.bfloat16), grad_input, grad_weight, grad_bias)


def solution(mesh):
    placed = (
        P("feat", "dom"),
        P(None, "feat"),
        P("feat"),
        P("dom", None, None),
        P("dom"),
        P("dom"),
        P("dom"),
        P("dom"),
        P("feat", "dom"),
    )
    return jax.shard_map(
        per_device,
        mesh=mesh,
        in_specs=placed,
        out_specs=(P("feat", "dom"), P("feat", "dom"), P(None, "feat"), P("feat")),
        check_vma=False,
    )
```

```python
import math

import jax
import jax.numpy as jnp
from jax import lax
from jax.sharding import PartitionSpec as P


def smooth_gate(values):
    return jax.nn.gelu(values, approximate=True)


def group_stack(values, axis, size, stride, count):
    received = [values]
    for offset in range(1, count):
        pairs = [(i, i ^ (offset * stride)) for i in range(size)]
        received.append(lax.ppermute(values, axis, pairs))
    stacked = jnp.stack(received)
    mine = (lax.axis_index(axis) // stride) % count
    return jnp.take(stacked, mine ^ jnp.arange(count), axis=0, mode="clip")


def exchange_order(values, axis, size, count, dim=0):
    received = [values]
    for offset in range(1, count):
        pairs = [(i, i ^ offset) for i in range(size)]
        received.append(lax.ppermute(values, axis, pairs))
    return received


def scatter_gather_sum(values, axis, size):
    rows, cols = values.shape
    chunk = rows // size
    gathered = lax.all_to_all(values.reshape(size, chunk, cols), axis, 0, 0, tiled=True)
    reduced = jnp.sum(gathered, axis=0)
    spread = jnp.broadcast_to(reduced[None], (size, chunk, cols))
    total = lax.all_to_all(spread, axis, 0, 0, tiled=True)
    return total.reshape(rows, cols)


def per_device(
    node_feats, weight, bias_vec, adj_tiles, tile_row, tile_col, tile_count, send_block, cotangent
):
    feat_rows, node_rows = node_feats.shape
    tile_slots = adj_tiles.shape[0]
    tile_size = adj_tiles.shape[1]
    blocks = node_rows // tile_size
    domains = lax.axis_size("dom")
    parts = lax.axis_size("feat")
    live_tiles = jnp.arange(tile_slots) < tile_count[0]
    slot_hit = jnp.logical_and(
        tile_col[:, None] == blocks + jnp.arange(domains)[None, :], live_tiles[:, None]
    )
    hit_tile = jnp.sum(jnp.where(slot_hit, jnp.arange(tile_slots)[:, None], 0), axis=0)
    has_hit = jnp.any(slot_hit, axis=0)
    slot_rows = jnp.sum(jnp.where(slot_hit, tile_row[:, None], 0), axis=0)
    peer_tiles = jnp.where(
        has_hit[:, None, None],
        jnp.take(adj_tiles, hit_tile, axis=0, mode="clip"),
        jnp.zeros((), adj_tiles.dtype),
    )
    order = lax.axis_index("feat") ^ jnp.arange(parts)
    pieces = exchange_order(node_feats, "feat", parts, parts)
    in_rows = weight.shape[0] // parts
    weight_ordered = jnp.take(
        weight.reshape(parts, in_rows, weight.shape[1]), order, axis=0, mode="clip"
    )
    hidden = sum(
        lax.dot_general(
            weight_ordered[s], piece, (((0,), (0,)), ((), ())), preferred_element_type=jnp.float32
        )
        for s, piece in enumerate(pieces)
    ).astype(jnp.bfloat16)
    hid_blocks = hidden.reshape(feat_rows, blocks, tile_size)
    outgoing = jnp.take(hid_blocks, send_block, axis=1, mode="clip")
    incoming = lax.all_to_all(outgoing, "dom", split_axis=1, concat_axis=1, tiled=True)
    live_float = live_tiles.astype(jnp.float32)
    local_ok = jnp.logical_and(live_tiles, tile_col < blocks).astype(jnp.float32)
    row_place = (tile_row[:, None] == jnp.arange(blocks)[None, :]).astype(jnp.float32) * local_ok[
        :, None
    ]
    picked = jnp.take(hid_blocks, jnp.minimum(tile_col, blocks - 1), axis=1, mode="clip")
    products = jnp.einsum("otb,tab->ota", picked, adj_tiles, preferred_element_type=jnp.float32)
    summed_local = jnp.einsum("ota,tr->ora", products, row_place, precision=lax.Precision.HIGHEST)
    summed_local, incoming = lax.optimization_barrier((summed_local, incoming))
    far_place = (slot_rows[:, None] == jnp.arange(blocks)[None, :]).astype(jnp.float32) * has_hit[
        :, None
    ].astype(jnp.float32)
    far_products = jnp.einsum(
        "oqb,qab->oqa", incoming, peer_tiles, preferred_element_type=jnp.float32
    )
    summed_far = jnp.einsum("oqa,qr->ora", far_products, far_place, precision=lax.Precision.HIGHEST)
    summed = (summed_local + summed_far).reshape(feat_rows, node_rows)
    preact = summed + bias_vec.astype(jnp.float32)[:, None]
    activated, pullback = jax.vjp(smooth_gate, preact)
    grad_pre = pullback(cotangent.astype(jnp.float32))[0]
    grad_low = grad_pre.astype(jnp.bfloat16)
    grad_blocks = grad_low.reshape(feat_rows, blocks, tile_size)
    rows_picked = jnp.take(grad_blocks, tile_row, axis=1, mode="clip")
    backward = jnp.einsum(
        "ota,tab->otb", rows_picked, adj_tiles, preferred_element_type=jnp.float32
    )
    src_place = (tile_col[:, None] == jnp.arange(blocks)[None, :]).astype(
        jnp.float32
    ) * live_float[:, None]
    recv_place = (send_block[:, None] == jnp.arange(blocks)[None, :]).astype(jnp.float32)
    own_sum = jnp.einsum(
        "otb,tr->orb", backward, src_place, precision=lax.Precision.HIGHEST
    )
    out_rows = jnp.take(grad_blocks, slot_rows, axis=1, mode="clip")
    out_parts = jnp.einsum(
        "oqa,qab->oqb", out_rows, peer_tiles, preferred_element_type=jnp.float32
    ).astype(jnp.bfloat16)
    in_parts = lax.all_to_all(out_parts, "dom", split_axis=1, concat_axis=1, tiled=True)
    late_weight, out_parts = lax.optimization_barrier((weight, out_parts))
    full_weight = jnp.concatenate(exchange_order(late_weight, "feat", parts, parts), axis=1)
    full_weight, in_parts = lax.optimization_barrier((full_weight, in_parts))
    remote_sum = in_parts.astype(jnp.float32)
    grad_sum = own_sum + jnp.einsum(
        "oqb,qr->orb", remote_sum, recv_place, precision=lax.Precision.HIGHEST
    )
    grad_hidden = grad_sum.reshape(feat_rows, node_rows).astype(jnp.bfloat16)
    norm_scale = 1.0 / math.sqrt(domains * node_rows)
    weight_part = jnp.concatenate(
        [
            lax.dot_general(
                grad_hidden, piece, (((1,), (1,)), ((), ())), preferred_element_type=jnp.float32
            )
            for piece in pieces
        ],
        axis=1,
    )
    bias_part = jnp.sum(grad_pre, axis=1)
    lanes = 128
    weight_rows = weight_part.size // lanes
    pack_rows = -(-(weight_rows + 1) // domains) * domains
    packed = jnp.zeros((pack_rows, lanes), jnp.float32)
    packed = packed.at[:weight_rows].set(weight_part.reshape(weight_rows, lanes))
    packed = packed.at[weight_rows, : bias_part.shape[0]].set(bias_part)
    packed = scatter_gather_sum(packed, "dom", domains)
    summed_weight = packed[:weight_rows].reshape(feat_rows, parts, in_rows)
    summed_weight = jnp.take(summed_weight, order, axis=1, mode="clip").reshape(feat_rows, parts * in_rows)
    grad_weight = summed_weight.T * norm_scale
    grad_bias = packed[weight_rows, : bias_part.shape[0]] * norm_scale
    all_grad = jnp.concatenate(exchange_order(grad_hidden, "feat", parts, parts), axis=0)
    my_rows = lax.dynamic_slice_in_dim(
        full_weight, lax.axis_index("feat") * feat_rows, feat_rows, 0
    )
    grad_input = jnp.dot(my_rows, all_grad, preferred_element_type=jnp.float32).astype(jnp.bfloat16)
    return (activated.astype(jnp.bfloat16), grad_input, grad_weight, grad_bias)


def solution(mesh):
    placed = (
        P("feat", "dom"),
        P(None, "feat"),
        P("feat"),
        P("dom", None, None),
        P("dom"),
        P("dom"),
        P("dom"),
        P("dom"),
        P("feat", "dom"),
    )
    return jax.shard_map(
        per_device,
        mesh=mesh,
        in_specs=placed,
        out_specs=(P("feat", "dom"), P("feat", "dom"), P(None, "feat"), P("feat")),
        check_vma=False,
    )
```

```python
import math

import jax
import jax.numpy as jnp
from jax import lax
from jax.sharding import PartitionSpec as P


def smooth_gate(values):
    return jax.nn.gelu(values, approximate=True)


def group_stack(values, axis, size, stride, count):
    received = [values]
    for offset in range(1, count):
        pairs = [(i, i ^ (offset * stride)) for i in range(size)]
        received.append(lax.ppermute(values, axis, pairs))
    stacked = jnp.stack(received)
    mine = (lax.axis_index(axis) // stride) % count
    return jnp.take(stacked, mine ^ jnp.arange(count), axis=0, mode="clip")


def exchange_order(values, axis, size, count, dim=0):
    received = [values]
    for offset in range(1, count):
        pairs = [(i, i ^ offset) for i in range(size)]
        received.append(lax.ppermute(values, axis, pairs))
    return received


def scatter_gather_sum(values, axis, size, rider):
    rows, cols = values.shape
    chunk = rows // size
    gathered = lax.all_to_all(values.reshape(size, chunk, cols), axis, 0, 0, tiled=True)
    reduced = jnp.sum(gathered, axis=0)
    reduced, rider = lax.optimization_barrier((reduced, rider))
    spread = jnp.broadcast_to(reduced[None], (size, chunk, cols))
    total = lax.all_to_all(spread, axis, 0, 0, tiled=True)
    return total.reshape(rows, cols), rider


def per_device(
    node_feats, weight, bias_vec, adj_tiles, tile_row, tile_col, tile_count, send_block, cotangent
):
    feat_rows, node_rows = node_feats.shape
    tile_slots = adj_tiles.shape[0]
    tile_size = adj_tiles.shape[1]
    blocks = node_rows // tile_size
    domains = lax.axis_size("dom")
    parts = lax.axis_size("feat")
    live_tiles = jnp.arange(tile_slots) < tile_count[0]
    slot_hit = jnp.logical_and(
        tile_col[:, None] == blocks + jnp.arange(domains)[None, :], live_tiles[:, None]
    )
    hit_tile = jnp.sum(jnp.where(slot_hit, jnp.arange(tile_slots)[:, None], 0), axis=0)
    has_hit = jnp.any(slot_hit, axis=0)
    slot_rows = jnp.sum(jnp.where(slot_hit, tile_row[:, None], 0), axis=0)
    peer_tiles = jnp.where(
        has_hit[:, None, None],
        jnp.take(adj_tiles, hit_tile, axis=0, mode="clip"),
        jnp.zeros((), adj_tiles.dtype),
    )
    order = lax.axis_index("feat") ^ jnp.arange(parts)
    pieces = exchange_order(node_feats, "feat", parts, parts)
    in_rows = weight.shape[0] // parts
    weight_ordered = jnp.take(
        weight.reshape(parts, in_rows, weight.shape[1]), order, axis=0, mode="clip"
    )
    hidden = sum(
        lax.dot_general(
            weight_ordered[s], piece, (((0,), (0,)), ((), ())), preferred_element_type=jnp.float32
        )
        for s, piece in enumerate(pieces)
    ).astype(jnp.bfloat16)
    hid_blocks = hidden.reshape(feat_rows, blocks, tile_size)
    outgoing = jnp.take(hid_blocks, send_block, axis=1, mode="clip")
    incoming = lax.all_to_all(outgoing, "dom", split_axis=1, concat_axis=1, tiled=True)
    live_float = live_tiles.astype(jnp.float32)
    local_ok = jnp.logical_and(live_tiles, tile_col < blocks).astype(jnp.float32)
    row_place = (tile_row[:, None] == jnp.arange(blocks)[None, :]).astype(jnp.float32) * local_ok[
        :, None
    ]
    picked = jnp.take(hid_blocks, jnp.minimum(tile_col, blocks - 1), axis=1, mode="clip")
    products = jnp.einsum("otb,tab->ota", picked, adj_tiles, preferred_element_type=jnp.float32)
    summed_local = jnp.einsum("ota,tr->ora", products, row_place, precision=lax.Precision.HIGHEST)
    whole = jnp.concatenate(pieces, axis=0)
    summed_local, whole, incoming = lax.optimization_barrier((summed_local, whole, incoming))
    far_place = (slot_rows[:, None] == jnp.arange(blocks)[None, :]).astype(jnp.float32) * has_hit[
        :, None
    ].astype(jnp.float32)
    far_products = jnp.einsum(
        "oqb,qab->oqa", incoming, peer_tiles, preferred_element_type=jnp.float32
    )
    summed_far = jnp.einsum("oqa,qr->ora", far_products, far_place, precision=lax.Precision.HIGHEST)
    summed = (summed_local + summed_far).reshape(feat_rows, node_rows)
    preact = summed + bias_vec.astype(jnp.float32)[:, None]
    activated, pullback = jax.vjp(smooth_gate, preact)
    grad_pre = pullback(cotangent.astype(jnp.float32))[0]
    grad_low = grad_pre.astype(jnp.bfloat16)
    grad_blocks = grad_low.reshape(feat_rows, blocks, tile_size)
    rows_picked = jnp.take(grad_blocks, tile_row, axis=1, mode="clip")
    backward = jnp.einsum(
        "ota,tab->otb", rows_picked, adj_tiles, preferred_element_type=jnp.float32
    )
    src_place = (tile_col[:, None] == jnp.arange(blocks)[None, :]).astype(
        jnp.float32
    ) * live_float[:, None]
    recv_place = (send_block[:, None] == jnp.arange(blocks)[None, :]).astype(jnp.float32)
    own_sum = jnp.einsum(
        "otb,tr->orb", backward, src_place, precision=lax.Precision.HIGHEST
    )
    out_rows = jnp.take(grad_blocks, slot_rows, axis=1, mode="clip")
    out_parts = jnp.einsum(
        "oqa,qab->oqb", out_rows, peer_tiles, preferred_element_type=jnp.float32
    ).astype(jnp.bfloat16)
    in_parts = lax.all_to_all(out_parts, "dom", split_axis=1, concat_axis=1, tiled=True)
    late_weight, out_parts = lax.optimization_barrier((weight, out_parts))
    full_weight = jnp.concatenate(exchange_order(late_weight, "feat", parts, parts), axis=1)
    full_weight, in_parts = lax.optimization_barrier((full_weight, in_parts))
    remote_sum = in_parts.astype(jnp.float32)
    grad_sum = own_sum + jnp.einsum(
        "oqb,qr->orb", remote_sum, recv_place, precision=lax.Precision.HIGHEST
    )
    grad_hidden = grad_sum.reshape(feat_rows, node_rows).astype(jnp.bfloat16)
    norm_scale = 1.0 / math.sqrt(domains * node_rows)
    weight_part = lax.dot_general(
        grad_hidden, whole, (((1,), (1,)), ((), ())), preferred_element_type=jnp.float32
    )
    bias_part = jnp.sum(grad_pre, axis=1)
    lanes = 128
    weight_rows = weight_part.size // lanes
    pack_rows = -(-(weight_rows + 1) // domains) * domains
    packed = jnp.zeros((pack_rows, lanes), jnp.float32)
    packed = packed.at[:weight_rows].set(weight_part.reshape(weight_rows, lanes))
    packed = packed.at[weight_rows, : bias_part.shape[0]].set(bias_part)
    packed, late_grad = scatter_gather_sum(packed, "dom", domains, grad_hidden)
    summed_weight = packed[:weight_rows].reshape(feat_rows, parts, in_rows)
    summed_weight = jnp.take(summed_weight, order, axis=1, mode="clip").reshape(feat_rows, parts * in_rows)
    grad_weight = summed_weight.T * norm_scale
    grad_bias = packed[weight_rows, : bias_part.shape[0]] * norm_scale
    all_grad = jnp.concatenate(exchange_order(late_grad, "feat", parts, parts), axis=0)
    my_rows = lax.dynamic_slice_in_dim(
        full_weight, lax.axis_index("feat") * feat_rows, feat_rows, 0
    )
    grad_input = jnp.dot(my_rows, all_grad, preferred_element_type=jnp.float32).astype(jnp.bfloat16)
    return (activated.astype(jnp.bfloat16), grad_input, grad_weight, grad_bias)


def solution(mesh):
    placed = (
        P("feat", "dom"),
        P(None, "feat"),
        P("feat"),
        P("dom", None, None),
        P("dom"),
        P("dom"),
        P("dom"),
        P("dom"),
        P("feat", "dom"),
    )
    return jax.shard_map(
        per_device,
        mesh=mesh,
        in_specs=placed,
        out_specs=(P("feat", "dom"), P("feat", "dom"), P(None, "feat"), P("feat")),
        check_vma=False,
    )
```

```python
import math

import jax
import jax.numpy as jnp
from jax import lax
from jax.sharding import PartitionSpec as P


def smooth_gate(values):
    return jax.nn.gelu(values, approximate=True)


def group_stack(values, axis, size, stride, count):
    received = [values]
    for offset in range(1, count):
        pairs = [(i, i ^ (offset * stride)) for i in range(size)]
        received.append(lax.ppermute(values, axis, pairs))
    stacked = jnp.stack(received)
    mine = (lax.axis_index(axis) // stride) % count
    return jnp.take(stacked, mine ^ jnp.arange(count), axis=0, mode="clip")


def exchange_order(values, axis, size, count, dim=0):
    received = [values]
    for offset in range(1, count):
        pairs = [(i, i ^ offset) for i in range(size)]
        received.append(lax.ppermute(values, axis, pairs))
    return received


def scatter_gather_sum(values, axis, size, rider):
    rows, cols = values.shape
    chunk = rows // size
    gathered = lax.all_to_all(values.reshape(size, chunk, cols), axis, 0, 0, tiled=True)
    reduced = jnp.sum(gathered, axis=0)
    reduced, rider = lax.optimization_barrier((reduced, rider))
    spread = jnp.broadcast_to(reduced[None], (size, chunk, cols))
    total = lax.all_to_all(spread, axis, 0, 0, tiled=True)
    return total.reshape(rows, cols), rider


def per_device(
    node_feats, weight, bias_vec, adj_tiles, tile_row, tile_col, tile_count, send_block, cotangent
):
    feat_rows, node_rows = node_feats.shape
    tile_slots = adj_tiles.shape[0]
    tile_size = adj_tiles.shape[1]
    blocks = node_rows // tile_size
    domains = lax.axis_size("dom")
    parts = lax.axis_size("feat")
    live_tiles = jnp.arange(tile_slots) < tile_count[0]
    slot_hit = jnp.logical_and(
        tile_col[:, None] == blocks + jnp.arange(domains)[None, :], live_tiles[:, None]
    )
    hit_tile = jnp.sum(jnp.where(slot_hit, jnp.arange(tile_slots)[:, None], 0), axis=0)
    has_hit = jnp.any(slot_hit, axis=0)
    slot_rows = jnp.sum(jnp.where(slot_hit, tile_row[:, None], 0), axis=0)
    peer_tiles = jnp.where(
        has_hit[:, None, None],
        jnp.take(adj_tiles, hit_tile, axis=0, mode="clip"),
        jnp.zeros((), adj_tiles.dtype),
    )
    order = lax.axis_index("feat") ^ jnp.arange(parts)
    pieces = exchange_order(node_feats, "feat", parts, parts)
    in_rows = weight.shape[0] // parts
    weight_ordered = jnp.take(
        weight.reshape(parts, in_rows, weight.shape[1]), order, axis=0, mode="clip"
    )
    hidden = sum(
        lax.dot_general(
            weight_ordered[s], piece, (((0,), (0,)), ((), ())), preferred_element_type=jnp.float32
        )
        for s, piece in enumerate(pieces)
    ).astype(jnp.bfloat16)
    hid_blocks = hidden.reshape(feat_rows, blocks, tile_size)
    outgoing = jnp.take(hid_blocks, send_block, axis=1, mode="clip")
    incoming = lax.all_to_all(outgoing, "dom", split_axis=1, concat_axis=1, tiled=True)
    live_float = live_tiles.astype(jnp.float32)
    local_ok = jnp.logical_and(live_tiles, tile_col < blocks).astype(jnp.float32)
    row_place = (tile_row[:, None] == jnp.arange(blocks)[None, :]).astype(jnp.float32) * local_ok[
        :, None
    ]
    picked = jnp.take(hid_blocks, jnp.minimum(tile_col, blocks - 1), axis=1, mode="clip")
    products = jnp.einsum("otb,tab->ota", picked, adj_tiles, preferred_element_type=jnp.float32)
    summed_local = jnp.einsum("ota,tr->ora", products, row_place, precision=lax.Precision.HIGHEST)
    whole = jnp.concatenate(pieces, axis=0)
    summed_local, whole, incoming = lax.optimization_barrier((summed_local, whole, incoming))
    far_place = (slot_rows[:, None] == jnp.arange(blocks)[None, :]).astype(jnp.float32) * has_hit[
        :, None
    ].astype(jnp.float32)
    far_products = jnp.einsum(
        "oqb,qab->oqa", incoming, peer_tiles, preferred_element_type=jnp.float32
    )
    summed_far = jnp.einsum("oqa,qr->ora", far_products, far_place, precision=lax.Precision.HIGHEST)
    summed = (summed_local + summed_far).reshape(feat_rows, node_rows)
    preact = summed + bias_vec.astype(jnp.float32)[:, None]
    activated, pullback = jax.vjp(smooth_gate, preact)
    grad_pre = pullback(cotangent.astype(jnp.float32))[0]
    grad_low = grad_pre.astype(jnp.bfloat16)
    grad_blocks = grad_low.reshape(feat_rows, blocks, tile_size)
    rows_picked = jnp.take(grad_blocks, tile_row, axis=1, mode="clip")
    backward = jnp.einsum(
        "ota,tab->otb", rows_picked, adj_tiles, preferred_element_type=jnp.float32
    )
    src_place = (tile_col[:, None] == jnp.arange(blocks)[None, :]).astype(
        jnp.float32
    ) * live_float[:, None]
    recv_place = (send_block[:, None] == jnp.arange(blocks)[None, :]).astype(jnp.float32)
    own_sum = jnp.einsum(
        "otb,tr->orb", backward, src_place, precision=lax.Precision.HIGHEST
    )
    out_rows = jnp.take(grad_blocks, slot_rows, axis=1, mode="clip")
    out_parts = jnp.einsum(
        "oqa,qab->oqb", out_rows, peer_tiles, preferred_element_type=jnp.float32
    ).astype(jnp.bfloat16)
    in_parts = lax.all_to_all(out_parts, "dom", split_axis=1, concat_axis=1, tiled=True)
    late_weight, out_parts = lax.optimization_barrier((weight, out_parts))
    full_weight = jnp.concatenate(exchange_order(late_weight, "feat", parts, parts), axis=1)
    full_weight, in_parts = lax.optimization_barrier((full_weight, in_parts))
    grad_sum = own_sum + jnp.einsum(
        "oqb,qr->orb", in_parts, recv_place.astype(jnp.bfloat16), preferred_element_type=jnp.float32
    )
    grad_hidden = grad_sum.reshape(feat_rows, node_rows).astype(jnp.bfloat16)
    norm_scale = 1.0 / math.sqrt(domains * node_rows)
    weight_part = lax.dot_general(
        grad_hidden, whole, (((1,), (1,)), ((), ())), preferred_element_type=jnp.float32
    )
    bias_part = jnp.sum(grad_pre, axis=1)
    lanes = 128
    weight_rows = weight_part.size // lanes
    pack_rows = -(-(weight_rows + 1) // domains) * domains
    packed = jnp.zeros((pack_rows, lanes), jnp.float32)
    packed = packed.at[:weight_rows].set(weight_part.reshape(weight_rows, lanes))
    packed = packed.at[weight_rows, : bias_part.shape[0]].set(bias_part)
    packed, late_grad = scatter_gather_sum(packed, "dom", domains, grad_hidden)
    summed_weight = packed[:weight_rows].reshape(feat_rows, parts, in_rows)
    summed_weight = jnp.take(summed_weight, order, axis=1, mode="clip").reshape(feat_rows, parts * in_rows)
    grad_weight = summed_weight.T * norm_scale
    grad_bias = packed[weight_rows, : bias_part.shape[0]] * norm_scale
    grad_pieces = [grad_hidden]
    for offset in range(1, parts):
        source = grad_hidden if offset in (1, parts - 1) else late_grad
        pairs = [(i, i ^ offset) for i in range(parts)]
        grad_pieces.append(lax.ppermute(source, "feat", pairs))
    all_grad = jnp.concatenate(grad_pieces, axis=0)
    my_rows = lax.dynamic_slice_in_dim(
        full_weight, lax.axis_index("feat") * feat_rows, feat_rows, 0
    )
    grad_input = jnp.dot(my_rows, all_grad, preferred_element_type=jnp.float32).astype(jnp.bfloat16)
    return (activated.astype(jnp.bfloat16), grad_input, grad_weight, grad_bias)


def solution(mesh):
    placed = (
        P("feat", "dom"),
        P(None, "feat"),
        P("feat"),
        P("dom", None, None),
        P("dom"),
        P("dom"),
        P("dom"),
        P("dom"),
        P("feat", "dom"),
    )
    return jax.shard_map(
        per_device,
        mesh=mesh,
        in_specs=placed,
        out_specs=(P("feat", "dom"), P("feat", "dom"), P(None, "feat"), P("feat")),
        check_vma=False,
    )
```

```python
import math

import jax
import jax.numpy as jnp
from jax import lax
from jax.sharding import PartitionSpec as P


def smooth_gate(values):
    return jax.nn.gelu(values, approximate=True)


def group_stack(values, axis, size, stride, count):
    received = [values]
    for offset in range(1, count):
        pairs = [(i, i ^ (offset * stride)) for i in range(size)]
        received.append(lax.ppermute(values, axis, pairs))
    stacked = jnp.stack(received)
    mine = (lax.axis_index(axis) // stride) % count
    return jnp.take(stacked, mine ^ jnp.arange(count), axis=0, mode="clip")


def exchange_order(values, axis, size, count, dim=0):
    received = [values]
    for offset in range(1, count):
        pairs = [(i, i ^ offset) for i in range(size)]
        received.append(lax.ppermute(values, axis, pairs))
    return received


def scatter_gather_sum(values, axis, size, rider):
    rows, cols = values.shape
    chunk = rows // size
    gathered = lax.all_to_all(values.reshape(size, chunk, cols), axis, 0, 0, tiled=True)
    reduced = jnp.sum(gathered, axis=0)
    reduced, rider = lax.optimization_barrier((reduced, rider))
    spread = jnp.broadcast_to(reduced[None], (size, chunk, cols))
    total = lax.all_to_all(spread, axis, 0, 0, tiled=True)
    return total.reshape(rows, cols), rider


def per_device(
    node_feats, weight, bias_vec, adj_tiles, tile_row, tile_col, tile_count, send_block, cotangent
):
    feat_rows, node_rows = node_feats.shape
    tile_slots = adj_tiles.shape[0]
    tile_size = adj_tiles.shape[1]
    blocks = node_rows // tile_size
    domains = lax.axis_size("dom")
    parts = lax.axis_size("feat")
    live_tiles = jnp.arange(tile_slots) < tile_count[0]
    slot_hit = jnp.logical_and(
        tile_col[:, None] == blocks + jnp.arange(domains)[None, :], live_tiles[:, None]
    )
    hit_tile = jnp.sum(jnp.where(slot_hit, jnp.arange(tile_slots)[:, None], 0), axis=0)
    has_hit = jnp.any(slot_hit, axis=0)
    slot_rows = jnp.sum(jnp.where(slot_hit, tile_row[:, None], 0), axis=0)
    peer_tiles = jnp.where(
        has_hit[:, None, None],
        jnp.take(adj_tiles, hit_tile, axis=0, mode="clip"),
        jnp.zeros((), adj_tiles.dtype),
    )
    order = lax.axis_index("feat") ^ jnp.arange(parts)
    pieces = exchange_order(node_feats, "feat", parts, parts)
    in_rows = weight.shape[0] // parts
    weight_ordered = jnp.take(
        weight.reshape(parts, in_rows, weight.shape[1]), order, axis=0, mode="clip"
    )
    hidden = sum(
        lax.dot_general(
            weight_ordered[s], piece, (((0,), (0,)), ((), ())), preferred_element_type=jnp.float32
        )
        for s, piece in enumerate(pieces)
    ).astype(jnp.bfloat16)
    hid_blocks = hidden.reshape(feat_rows, blocks, tile_size)
    outgoing = jnp.take(hid_blocks, send_block, axis=1, mode="clip")
    incoming = lax.all_to_all(outgoing, "dom", split_axis=1, concat_axis=1, tiled=True)
    live_float = live_tiles.astype(jnp.float32)
    local_ok = jnp.logical_and(live_tiles, tile_col < blocks).astype(jnp.float32)
    row_place = (tile_row[:, None] == jnp.arange(blocks)[None, :]).astype(jnp.float32) * local_ok[
        :, None
    ]
    picked = jnp.take(hid_blocks, jnp.minimum(tile_col, blocks - 1), axis=1, mode="clip")
    products = jnp.einsum("otb,tab->ota", picked, adj_tiles, preferred_element_type=jnp.float32)
    summed_local = jnp.einsum("ota,tr->ora", products, row_place, precision=lax.Precision.HIGHEST)
    whole = jnp.concatenate(pieces, axis=0)
    summed_local, whole, incoming = lax.optimization_barrier((summed_local, whole, incoming))
    far_place = (slot_rows[:, None] == jnp.arange(blocks)[None, :]).astype(jnp.float32) * has_hit[
        :, None
    ].astype(jnp.float32)
    far_products = jnp.einsum(
        "oqb,qab->oqa", incoming, peer_tiles, preferred_element_type=jnp.float32
    )
    far_hi = far_products.astype(jnp.bfloat16)
    far_rest = far_products - far_hi.astype(jnp.float32)
    far_mid = far_rest.astype(jnp.bfloat16)
    far_lo = (far_rest - far_mid.astype(jnp.float32)).astype(jnp.bfloat16)
    far_place_low = far_place.astype(jnp.bfloat16)
    summed_far = sum(
        jnp.einsum("oqa,qr->ora", part, far_place_low, preferred_element_type=jnp.float32)
        for part in (far_hi, far_mid, far_lo)
    )
    summed = (summed_local + summed_far).reshape(feat_rows, node_rows)
    preact = summed + bias_vec.astype(jnp.float32)[:, None]
    activated, pullback = jax.vjp(smooth_gate, preact)
    grad_pre = pullback(cotangent.astype(jnp.float32))[0]
    grad_low = grad_pre.astype(jnp.bfloat16)
    grad_blocks = grad_low.reshape(feat_rows, blocks, tile_size)
    rows_picked = jnp.take(grad_blocks, tile_row, axis=1, mode="clip")
    backward = jnp.einsum(
        "ota,tab->otb", rows_picked, adj_tiles, preferred_element_type=jnp.float32
    )
    src_place = (tile_col[:, None] == jnp.arange(blocks)[None, :]).astype(
        jnp.float32
    ) * live_float[:, None]
    recv_place = (send_block[:, None] == jnp.arange(blocks)[None, :]).astype(jnp.float32)
    own_sum = jnp.einsum(
        "otb,tr->orb", backward, src_place, precision=lax.Precision.HIGHEST
    )
    out_rows = jnp.take(grad_blocks, slot_rows, axis=1, mode="clip")
    out_parts = jnp.einsum(
        "oqa,qab->oqb", out_rows, peer_tiles, preferred_element_type=jnp.float32
    ).astype(jnp.bfloat16)
    in_parts = lax.all_to_all(out_parts, "dom", split_axis=1, concat_axis=1, tiled=True)
    late_weight, out_parts = lax.optimization_barrier((weight, out_parts))
    full_weight = jnp.concatenate(exchange_order(late_weight, "feat", parts, parts), axis=1)
    full_weight, in_parts = lax.optimization_barrier((full_weight, in_parts))
    grad_sum = own_sum + jnp.einsum(
        "oqb,qr->orb", in_parts, recv_place.astype(jnp.bfloat16), preferred_element_type=jnp.float32
    )
    grad_hidden = grad_sum.reshape(feat_rows, node_rows).astype(jnp.bfloat16)
    norm_scale = 1.0 / math.sqrt(domains * node_rows)
    weight_part = lax.dot_general(
        grad_hidden, whole, (((1,), (1,)), ((), ())), preferred_element_type=jnp.float32
    )
    bias_part = jnp.sum(grad_pre, axis=1)
    lanes = 128
    weight_rows = weight_part.size // lanes
    pack_rows = -(-(weight_rows + 1) // domains) * domains
    packed = jnp.zeros((pack_rows, lanes), jnp.float32)
    packed = packed.at[:weight_rows].set(weight_part.reshape(weight_rows, lanes))
    packed = packed.at[weight_rows, : bias_part.shape[0]].set(bias_part)
    packed, late_grad = scatter_gather_sum(packed, "dom", domains, grad_hidden)
    summed_weight = packed[:weight_rows].reshape(feat_rows, parts, in_rows)
    summed_weight = jnp.take(summed_weight, order, axis=1, mode="clip").reshape(feat_rows, parts * in_rows)
    grad_weight = summed_weight.T * norm_scale
    grad_bias = packed[weight_rows, : bias_part.shape[0]] * norm_scale
    grad_pieces = [grad_hidden]
    for offset in range(1, parts):
        source = grad_hidden if offset in (1, parts - 1) else late_grad
        pairs = [(i, i ^ offset) for i in range(parts)]
        grad_pieces.append(lax.ppermute(source, "feat", pairs))
    all_grad = jnp.concatenate(grad_pieces, axis=0)
    my_rows = lax.dynamic_slice_in_dim(
        full_weight, lax.axis_index("feat") * feat_rows, feat_rows, 0
    )
    grad_input = jnp.dot(my_rows, all_grad, preferred_element_type=jnp.float32).astype(jnp.bfloat16)
    return (activated.astype(jnp.bfloat16), grad_input, grad_weight, grad_bias)


def solution(mesh):
    placed = (
        P("feat", "dom"),
        P(None, "feat"),
        P("feat"),
        P("dom", None, None),
        P("dom"),
        P("dom"),
        P("dom"),
        P("dom"),
        P("feat", "dom"),
    )
    return jax.shard_map(
        per_device,
        mesh=mesh,
        in_specs=placed,
        out_specs=(P("feat", "dom"), P("feat", "dom"), P(None, "feat"), P("feat")),
        check_vma=False,
    )
```

```python
import math

import jax
import jax.numpy as jnp
from jax import lax
from jax.sharding import PartitionSpec as P


def smooth_gate(values):
    return jax.nn.gelu(values, approximate=True)


def group_stack(values, axis, size, stride, count):
    received = [values]
    for offset in range(1, count):
        pairs = [(i, i ^ (offset * stride)) for i in range(size)]
        received.append(lax.ppermute(values, axis, pairs))
    stacked = jnp.stack(received)
    mine = (lax.axis_index(axis) // stride) % count
    return jnp.take(stacked, mine ^ jnp.arange(count), axis=0, mode="clip")


def exchange_order(values, axis, size, count, dim=0):
    received = [values]
    for offset in range(1, count):
        pairs = [(i, i ^ offset) for i in range(size)]
        received.append(lax.ppermute(values, axis, pairs))
    return received


def scatter_gather_sum(values, axis, size, rider):
    rows, cols = values.shape
    chunk = rows // size
    gathered = lax.all_to_all(values.reshape(size, chunk, cols), axis, 0, 0, tiled=True)
    reduced = jnp.sum(gathered, axis=0)
    reduced, rider = lax.optimization_barrier((reduced, rider))
    spread = jnp.broadcast_to(reduced[None], (size, chunk, cols))
    total = lax.all_to_all(spread, axis, 0, 0, tiled=True)
    return total.reshape(rows, cols), rider


def neighbour_order(values, axis, count):
    if count != 4:
        return exchange_order(values, axis, count, count)
    pairs = lambda offset: [(i, i ^ offset) for i in range(count)]
    first = lax.ppermute(values, axis, pairs(1))
    third = lax.ppermute(values, axis, pairs(3))
    second = lax.ppermute(first, axis, pairs(3))
    return [values, first, second, third]


def per_device(
    node_feats, weight, bias_vec, adj_tiles, tile_row, tile_col, tile_count, send_block, cotangent
):
    feat_rows, node_rows = node_feats.shape
    tile_slots = adj_tiles.shape[0]
    tile_size = adj_tiles.shape[1]
    blocks = node_rows // tile_size
    domains = lax.axis_size("dom")
    parts = lax.axis_size("feat")
    live_tiles = jnp.arange(tile_slots) < tile_count[0]
    slot_hit = jnp.logical_and(
        tile_col[:, None] == blocks + jnp.arange(domains)[None, :], live_tiles[:, None]
    )
    hit_tile = jnp.sum(jnp.where(slot_hit, jnp.arange(tile_slots)[:, None], 0), axis=0)
    has_hit = jnp.any(slot_hit, axis=0)
    slot_rows = jnp.sum(jnp.where(slot_hit, tile_row[:, None], 0), axis=0)
    peer_tiles = jnp.where(
        has_hit[:, None, None],
        jnp.take(adj_tiles, hit_tile, axis=0, mode="clip"),
        jnp.zeros((), adj_tiles.dtype),
    )
    order = lax.axis_index("feat") ^ jnp.arange(parts)
    pieces = neighbour_order(node_feats, "feat", parts)
    in_rows = weight.shape[0] // parts
    weight_ordered = jnp.take(
        weight.reshape(parts, in_rows, weight.shape[1]), order, axis=0, mode="clip"
    )
    hidden = sum(
        lax.dot_general(
            weight_ordered[s], piece, (((0,), (0,)), ((), ())), preferred_element_type=jnp.float32
        )
        for s, piece in enumerate(pieces)
    ).astype(jnp.bfloat16)
    hid_blocks = hidden.reshape(feat_rows, blocks, tile_size)
    outgoing = jnp.take(hid_blocks, send_block, axis=1, mode="clip")
    incoming = lax.all_to_all(outgoing, "dom", split_axis=1, concat_axis=1, tiled=True)
    live_float = live_tiles.astype(jnp.float32)
    local_ok = jnp.logical_and(live_tiles, tile_col < blocks).astype(jnp.float32)
    row_place = (tile_row[:, None] == jnp.arange(blocks)[None, :]).astype(jnp.float32) * local_ok[
        :, None
    ]
    picked = jnp.take(hid_blocks, jnp.minimum(tile_col, blocks - 1), axis=1, mode="clip")
    products = jnp.einsum("otb,tab->ota", picked, adj_tiles, preferred_element_type=jnp.float32)
    summed_local = jnp.einsum("ota,tr->ora", products, row_place, precision=lax.Precision.HIGHEST)
    whole = jnp.concatenate(pieces, axis=0)
    summed_local, whole, incoming = lax.optimization_barrier((summed_local, whole, incoming))
    far_place = (slot_rows[:, None] == jnp.arange(blocks)[None, :]).astype(jnp.float32) * has_hit[
        :, None
    ].astype(jnp.float32)
    far_products = jnp.einsum(
        "oqb,qab->oqa", incoming, peer_tiles, preferred_element_type=jnp.float32
    )
    summed_far = jnp.einsum("oqa,qr->ora", far_products, far_place, precision=lax.Precision.HIGHEST)
    summed = (summed_local + summed_far).reshape(feat_rows, node_rows)
    preact = summed + bias_vec.astype(jnp.float32)[:, None]
    activated, pullback = jax.vjp(smooth_gate, preact)
    grad_pre = pullback(cotangent.astype(jnp.float32))[0]
    grad_low = grad_pre.astype(jnp.bfloat16)
    grad_blocks = grad_low.reshape(feat_rows, blocks, tile_size)
    rows_picked = jnp.take(grad_blocks, tile_row, axis=1, mode="clip")
    backward = jnp.einsum(
        "ota,tab->otb", rows_picked, adj_tiles, preferred_element_type=jnp.float32
    )
    src_place = (tile_col[:, None] == jnp.arange(blocks)[None, :]).astype(
        jnp.float32
    ) * live_float[:, None]
    recv_place = (send_block[:, None] == jnp.arange(blocks)[None, :]).astype(jnp.float32)
    own_sum = jnp.einsum(
        "otb,tr->orb", backward, src_place, precision=lax.Precision.HIGHEST
    )
    out_rows = jnp.take(grad_blocks, slot_rows, axis=1, mode="clip")
    out_parts = jnp.einsum(
        "oqa,qab->oqb", out_rows, peer_tiles, preferred_element_type=jnp.float32
    ).astype(jnp.bfloat16)
    in_parts = lax.all_to_all(out_parts, "dom", split_axis=1, concat_axis=1, tiled=True)
    late_weight, out_parts = lax.optimization_barrier((weight, out_parts))
    full_weight = jnp.concatenate(exchange_order(late_weight, "feat", parts, parts), axis=1)
    full_weight, in_parts = lax.optimization_barrier((full_weight, in_parts))
    grad_sum = own_sum + jnp.einsum(
        "oqb,qr->orb", in_parts, recv_place.astype(jnp.bfloat16), preferred_element_type=jnp.float32
    )
    grad_hidden = grad_sum.reshape(feat_rows, node_rows).astype(jnp.bfloat16)
    norm_scale = 1.0 / math.sqrt(domains * node_rows)
    weight_part = lax.dot_general(
        grad_hidden, whole, (((1,), (1,)), ((), ())), preferred_element_type=jnp.float32
    )
    bias_part = jnp.sum(grad_pre, axis=1)
    lanes = 128
    weight_rows = weight_part.size // lanes
    pack_rows = -(-(weight_rows + 1) // domains) * domains
    packed = jnp.zeros((pack_rows, lanes), jnp.float32)
    packed = packed.at[:weight_rows].set(weight_part.reshape(weight_rows, lanes))
    packed = packed.at[weight_rows, : bias_part.shape[0]].set(bias_part)
    packed, late_grad = scatter_gather_sum(packed, "dom", domains, grad_hidden)
    summed_weight = packed[:weight_rows].reshape(feat_rows, parts, in_rows)
    summed_weight = jnp.take(summed_weight, order, axis=1, mode="clip").reshape(feat_rows, parts * in_rows)
    grad_weight = summed_weight.T * norm_scale
    grad_bias = packed[weight_rows, : bias_part.shape[0]] * norm_scale
    grad_pieces = [grad_hidden]
    for offset in range(1, parts):
        source = grad_hidden if offset in (1, parts - 1) else late_grad
        pairs = [(i, i ^ offset) for i in range(parts)]
        grad_pieces.append(lax.ppermute(source, "feat", pairs))
    all_grad = jnp.concatenate(grad_pieces, axis=0)
    my_rows = lax.dynamic_slice_in_dim(
        full_weight, lax.axis_index("feat") * feat_rows, feat_rows, 0
    )
    grad_input = jnp.dot(my_rows, all_grad, preferred_element_type=jnp.float32).astype(jnp.bfloat16)
    return (activated.astype(jnp.bfloat16), grad_input, grad_weight, grad_bias)


def solution(mesh):
    placed = (
        P("feat", "dom"),
        P(None, "feat"),
        P("feat"),
        P("dom", None, None),
        P("dom"),
        P("dom"),
        P("dom"),
        P("dom"),
        P("feat", "dom"),
    )
    return jax.shard_map(
        per_device,
        mesh=mesh,
        in_specs=placed,
        out_specs=(P("feat", "dom"), P("feat", "dom"), P(None, "feat"), P("feat")),
        check_vma=False,
    )
```

```python
import math

import jax
import jax.numpy as jnp
from jax import lax
from jax.sharding import PartitionSpec as P


def smooth_gate(values):
    return jax.nn.gelu(values, approximate=True)


def group_stack(values, axis, size, stride, count):
    received = [values]
    for offset in range(1, count):
        pairs = [(i, i ^ (offset * stride)) for i in range(size)]
        received.append(lax.ppermute(values, axis, pairs))
    stacked = jnp.stack(received)
    mine = (lax.axis_index(axis) // stride) % count
    return jnp.take(stacked, mine ^ jnp.arange(count), axis=0, mode="clip")


def exchange_order(values, axis, size, count, dim=0):
    received = [values]
    for offset in range(1, count):
        pairs = [(i, i ^ offset) for i in range(size)]
        received.append(lax.ppermute(values, axis, pairs))
    return received


def scatter_gather_sum(values, axis, size, rider):
    rows, cols = values.shape
    chunk = rows // size
    gathered = lax.all_to_all(values.reshape(size, chunk, cols), axis, 0, 0, tiled=True)
    reduced = jnp.sum(gathered, axis=0)
    reduced, rider = lax.optimization_barrier((reduced, rider))
    spread = jnp.broadcast_to(reduced[None], (size, chunk, cols))
    total = lax.all_to_all(spread, axis, 0, 0, tiled=True)
    return total.reshape(rows, cols), rider


def per_device(
    node_feats, weight, bias_vec, adj_tiles, tile_row, tile_col, tile_count, send_block, cotangent
):
    feat_rows, node_rows = node_feats.shape
    tile_slots = adj_tiles.shape[0]
    tile_size = adj_tiles.shape[1]
    blocks = node_rows // tile_size
    domains = lax.axis_size("dom")
    parts = lax.axis_size("feat")
    live_tiles = jnp.arange(tile_slots) < tile_count[0]
    slot_hit = jnp.logical_and(
        tile_col[:, None] == blocks + jnp.arange(domains)[None, :], live_tiles[:, None]
    )
    hit_tile = jnp.sum(jnp.where(slot_hit, jnp.arange(tile_slots)[:, None], 0), axis=0)
    has_hit = jnp.any(slot_hit, axis=0)
    slot_rows = jnp.sum(jnp.where(slot_hit, tile_row[:, None], 0), axis=0)
    peer_tiles = jnp.where(
        has_hit[:, None, None],
        jnp.take(adj_tiles, hit_tile, axis=0, mode="clip"),
        jnp.zeros((), adj_tiles.dtype),
    )
    order = lax.axis_index("feat") ^ jnp.arange(parts)
    pieces = exchange_order(node_feats, "feat", parts, parts)
    in_rows = weight.shape[0] // parts
    weight_ordered = jnp.take(
        weight.reshape(parts, in_rows, weight.shape[1]), order, axis=0, mode="clip"
    )
    hidden = sum(
        lax.dot_general(
            weight_ordered[s], piece, (((0,), (0,)), ((), ())), preferred_element_type=jnp.float32
        )
        for s, piece in enumerate(pieces)
    ).astype(jnp.bfloat16)
    hid_blocks = hidden.reshape(feat_rows, blocks, tile_size)
    outgoing = jnp.take(hid_blocks, send_block, axis=1, mode="clip")
    incoming = lax.all_to_all(outgoing, "dom", split_axis=1, concat_axis=1, tiled=True)
    live_float = live_tiles.astype(jnp.float32)
    local_ok = jnp.logical_and(live_tiles, tile_col < blocks).astype(jnp.float32)
    row_place = (tile_row[:, None] == jnp.arange(blocks)[None, :]).astype(jnp.float32) * local_ok[
        :, None
    ]
    picked = jnp.take(hid_blocks, jnp.minimum(tile_col, blocks - 1), axis=1, mode="clip")
    products = jnp.einsum("otb,tab->ota", picked, adj_tiles, preferred_element_type=jnp.float32)
    summed_local = jnp.einsum("ota,tr->ora", products, row_place, precision=lax.Precision.HIGHEST)
    whole = jnp.concatenate(pieces, axis=0)
    summed_local, whole, incoming = lax.optimization_barrier((summed_local, whole, incoming))
    far_place = (slot_rows[:, None] == jnp.arange(blocks)[None, :]).astype(jnp.float32) * has_hit[
        :, None
    ].astype(jnp.float32)
    far_products = jnp.einsum(
        "oqb,qab->oqa", incoming, peer_tiles, preferred_element_type=jnp.float32
    )
    summed_far = jnp.einsum("oqa,qr->ora", far_products, far_place, precision=lax.Precision.HIGH)
    summed = (summed_local + summed_far).reshape(feat_rows, node_rows)
    preact = summed + bias_vec.astype(jnp.float32)[:, None]
    activated, pullback = jax.vjp(smooth_gate, preact)
    grad_pre = pullback(cotangent.astype(jnp.float32))[0]
    grad_low = grad_pre.astype(jnp.bfloat16)
    grad_blocks = grad_low.reshape(feat_rows, blocks, tile_size)
    rows_picked = jnp.take(grad_blocks, tile_row, axis=1, mode="clip")
    backward = jnp.einsum(
        "ota,tab->otb", rows_picked, adj_tiles, preferred_element_type=jnp.float32
    )
    src_place = (tile_col[:, None] == jnp.arange(blocks)[None, :]).astype(
        jnp.float32
    ) * live_float[:, None]
    recv_place = (send_block[:, None] == jnp.arange(blocks)[None, :]).astype(jnp.float32)
    own_sum = jnp.einsum(
        "otb,tr->orb", backward, src_place, precision=lax.Precision.HIGHEST
    )
    out_rows = jnp.take(grad_blocks, slot_rows, axis=1, mode="clip")
    out_parts = jnp.einsum(
        "oqa,qab->oqb", out_rows, peer_tiles, preferred_element_type=jnp.float32
    ).astype(jnp.bfloat16)
    in_parts = lax.all_to_all(out_parts, "dom", split_axis=1, concat_axis=1, tiled=True)
    late_weight, out_parts = lax.optimization_barrier((weight, out_parts))
    full_weight = jnp.concatenate(exchange_order(late_weight, "feat", parts, parts), axis=1)
    full_weight, in_parts = lax.optimization_barrier((full_weight, in_parts))
    grad_sum = own_sum + jnp.einsum(
        "oqb,qr->orb", in_parts, recv_place.astype(jnp.bfloat16), preferred_element_type=jnp.float32
    )
    grad_hidden = grad_sum.reshape(feat_rows, node_rows).astype(jnp.bfloat16)
    norm_scale = 1.0 / math.sqrt(domains * node_rows)
    weight_part = lax.dot_general(
        grad_hidden, whole, (((1,), (1,)), ((), ())), preferred_element_type=jnp.float32
    )
    bias_part = jnp.sum(grad_pre, axis=1)
    lanes = 128
    weight_rows = weight_part.size // lanes
    pack_rows = -(-(weight_rows + 1) // domains) * domains
    packed = jnp.zeros((pack_rows, lanes), jnp.float32)
    packed = packed.at[:weight_rows].set(weight_part.reshape(weight_rows, lanes))
    packed = packed.at[weight_rows, : bias_part.shape[0]].set(bias_part)
    packed, late_grad = scatter_gather_sum(packed, "dom", domains, grad_hidden)
    summed_weight = packed[:weight_rows].reshape(feat_rows, parts, in_rows)
    summed_weight = jnp.take(summed_weight, order, axis=1, mode="clip").reshape(feat_rows, parts * in_rows)
    grad_weight = summed_weight.T * norm_scale
    grad_bias = packed[weight_rows, : bias_part.shape[0]] * norm_scale
    grad_pieces = [grad_hidden]
    for offset in range(1, parts):
        source = grad_hidden if offset in (1, parts - 1) else late_grad
        pairs = [(i, i ^ offset) for i in range(parts)]
        grad_pieces.append(lax.ppermute(source, "feat", pairs))
    all_grad = jnp.concatenate(grad_pieces, axis=0)
    my_rows = lax.dynamic_slice_in_dim(
        full_weight, lax.axis_index("feat") * feat_rows, feat_rows, 0
    )
    grad_input = jnp.dot(my_rows, all_grad, preferred_element_type=jnp.float32).astype(jnp.bfloat16)
    return (activated.astype(jnp.bfloat16), grad_input, grad_weight, grad_bias)


def solution(mesh):
    placed = (
        P("feat", "dom"),
        P(None, "feat"),
        P("feat"),
        P("dom", None, None),
        P("dom"),
        P("dom"),
        P("dom"),
        P("dom"),
        P("feat", "dom"),
    )
    return jax.shard_map(
        per_device,
        mesh=mesh,
        in_specs=placed,
        out_specs=(P("feat", "dom"), P("feat", "dom"), P(None, "feat"), P("feat")),
        check_vma=False,
    )
```

```python
import math

import jax
import jax.numpy as jnp
from jax import lax
from jax.sharding import PartitionSpec as P


def smooth_gate(values):
    return jax.nn.gelu(values, approximate=True)


def group_stack(values, axis, size, stride, count):
    received = [values]
    for offset in range(1, count):
        pairs = [(i, i ^ (offset * stride)) for i in range(size)]
        received.append(lax.ppermute(values, axis, pairs))
    stacked = jnp.stack(received)
    mine = (lax.axis_index(axis) // stride) % count
    return jnp.take(stacked, mine ^ jnp.arange(count), axis=0, mode="clip")


def exchange_order(values, axis, size, count, dim=0):
    received = [values]
    for offset in range(1, count):
        pairs = [(i, i ^ offset) for i in range(size)]
        received.append(lax.ppermute(values, axis, pairs))
    return received


def scatter_gather_sum(values, axis, size, rider):
    rows, cols = values.shape
    chunk = rows // size
    gathered = lax.all_to_all(values.reshape(size, chunk, cols), axis, 0, 0, tiled=True)
    reduced = jnp.sum(gathered, axis=0)
    reduced, rider = lax.optimization_barrier((reduced, rider))
    spread = jnp.broadcast_to(reduced[None], (size, chunk, cols))
    total = lax.all_to_all(spread, axis, 0, 0, tiled=True)
    return total.reshape(rows, cols), rider


def per_device(
    node_feats, weight, bias_vec, adj_tiles, tile_row, tile_col, tile_count, send_block, cotangent
):
    feat_rows, node_rows = node_feats.shape
    tile_slots = adj_tiles.shape[0]
    tile_size = adj_tiles.shape[1]
    blocks = node_rows // tile_size
    domains = lax.axis_size("dom")
    parts = lax.axis_size("feat")
    live_tiles = jnp.arange(tile_slots) < tile_count[0]
    slot_hit = jnp.logical_and(
        tile_col[:, None] == blocks + jnp.arange(domains)[None, :], live_tiles[:, None]
    )
    hit_tile = jnp.sum(jnp.where(slot_hit, jnp.arange(tile_slots)[:, None], 0), axis=0)
    has_hit = jnp.any(slot_hit, axis=0)
    slot_rows = jnp.sum(jnp.where(slot_hit, tile_row[:, None], 0), axis=0)
    peer_tiles = jnp.where(
        has_hit[:, None, None],
        jnp.take(adj_tiles, hit_tile, axis=0, mode="clip"),
        jnp.zeros((), adj_tiles.dtype),
    )
    order = lax.axis_index("feat") ^ jnp.arange(parts)
    pieces = exchange_order(node_feats, "feat", parts, parts)
    in_rows = weight.shape[0] // parts
    weight_ordered = jnp.take(
        weight.reshape(parts, in_rows, weight.shape[1]), order, axis=0, mode="clip"
    )
    hidden = sum(
        lax.dot_general(
            weight_ordered[s], piece, (((0,), (0,)), ((), ())), preferred_element_type=jnp.float32
        )
        for s, piece in enumerate(pieces)
    ).astype(jnp.bfloat16)
    hid_blocks = hidden.reshape(feat_rows, blocks, tile_size)
    outgoing = jnp.take(hid_blocks, send_block, axis=1, mode="clip")
    incoming = lax.all_to_all(outgoing, "dom", split_axis=1, concat_axis=1, tiled=True)
    live_float = live_tiles.astype(jnp.float32)
    local_ok = jnp.logical_and(live_tiles, tile_col < blocks).astype(jnp.float32)
    row_place = (tile_row[:, None] == jnp.arange(blocks)[None, :]).astype(jnp.float32) * local_ok[
        :, None
    ]
    picked = jnp.take(hid_blocks, jnp.minimum(tile_col, blocks - 1), axis=1, mode="clip")
    products = jnp.einsum("otb,tab->ota", picked, adj_tiles, preferred_element_type=jnp.float32)
    summed_local = jnp.einsum("ota,tr->ora", products, row_place, precision=lax.Precision.HIGHEST)
    whole = jnp.concatenate(pieces, axis=0)
    summed_local, whole, incoming = lax.optimization_barrier((summed_local, whole, incoming))
    far_place = (slot_rows[:, None] == jnp.arange(blocks)[None, :]).astype(jnp.float32) * has_hit[
        :, None
    ].astype(jnp.float32)
    far_products = jnp.einsum(
        "oqb,qab->oqa", incoming, peer_tiles, preferred_element_type=jnp.float32
    )
    summed_far = jnp.einsum("oqa,qr->ora", far_products, far_place, precision=lax.Precision.HIGH)
    summed = (summed_local + summed_far).reshape(feat_rows, node_rows)
    preact = summed + bias_vec.astype(jnp.float32)[:, None]
    activated, pullback = jax.vjp(smooth_gate, preact)
    grad_pre = pullback(cotangent.astype(jnp.float32))[0]
    grad_low = grad_pre.astype(jnp.bfloat16)
    grad_blocks = grad_low.reshape(feat_rows, blocks, tile_size)
    rows_picked = jnp.take(grad_blocks, tile_row, axis=1, mode="clip")
    backward = jnp.einsum(
        "ota,tab->otb", rows_picked, adj_tiles, preferred_element_type=jnp.float32
    )
    src_place = (tile_col[:, None] == jnp.arange(blocks)[None, :]).astype(
        jnp.float32
    ) * live_float[:, None]
    recv_place = (send_block[:, None] == jnp.arange(blocks)[None, :]).astype(jnp.float32)
    own_sum = jnp.einsum(
        "otb,tr->orb", backward, src_place, precision=lax.Precision.HIGHEST
    )
    out_rows = jnp.take(grad_blocks, slot_rows, axis=1, mode="clip")
    out_parts = jnp.einsum(
        "oqa,qab->oqb", out_rows, peer_tiles, preferred_element_type=jnp.float32
    ).astype(jnp.bfloat16)
    in_parts = lax.all_to_all(out_parts, "dom", split_axis=1, concat_axis=1, tiled=True)
    late_weight, out_parts = lax.optimization_barrier((weight, out_parts))
    full_weight = jnp.concatenate(exchange_order(late_weight, "feat", parts, parts), axis=1)
    full_weight, in_parts = lax.optimization_barrier((full_weight, in_parts))
    grad_sum = own_sum + jnp.einsum(
        "oqb,qr->orb", in_parts, recv_place.astype(jnp.bfloat16), preferred_element_type=jnp.float32
    )
    grad_hidden = grad_sum.reshape(feat_rows, node_rows).astype(jnp.bfloat16)
    norm_scale = 1.0 / math.sqrt(domains * node_rows)
    weight_part = lax.dot_general(
        grad_hidden, whole, (((1,), (1,)), ((), ())), preferred_element_type=jnp.float32
    )
    bias_part = jnp.sum(grad_pre, axis=1)
    lanes = 128
    weight_rows = weight_part.size // lanes
    pack_rows = -(-(weight_rows + 1) // domains) * domains
    packed = jnp.zeros((pack_rows, lanes), jnp.float32)
    packed = packed.at[:weight_rows].set(weight_part.reshape(weight_rows, lanes))
    packed = packed.at[weight_rows, : bias_part.shape[0]].set(bias_part)
    packed, late_grad = scatter_gather_sum(packed, "dom", domains, grad_hidden)
    summed_weight = packed[:weight_rows].reshape(feat_rows, parts, in_rows)
    summed_weight = jnp.take(summed_weight, order, axis=1, mode="clip").reshape(feat_rows, parts * in_rows)
    grad_weight = summed_weight.T * norm_scale
    grad_bias = packed[weight_rows, : bias_part.shape[0]] * norm_scale
    grad_pieces = [grad_hidden]
    for offset in range(1, parts):
        source = grad_hidden if offset in (1, parts - 1) else late_grad
        pairs = [(i, i ^ offset) for i in range(parts)]
        grad_pieces.append(lax.ppermute(source, "feat", pairs))
    my_rows = lax.dynamic_slice_in_dim(
        full_weight, lax.axis_index("feat") * feat_rows, feat_rows, 0
    )
    grad_input = sum(
        jnp.dot(my_rows[:, s * feat_rows : (s + 1) * feat_rows], piece, preferred_element_type=jnp.float32)
        for s, piece in enumerate(grad_pieces)
    ).astype(jnp.bfloat16)
    return (activated.astype(jnp.bfloat16), grad_input, grad_weight, grad_bias)


def solution(mesh):
    placed = (
        P("feat", "dom"),
        P(None, "feat"),
        P("feat"),
        P("dom", None, None),
        P("dom"),
        P("dom"),
        P("dom"),
        P("dom"),
        P("feat", "dom"),
    )
    return jax.shard_map(
        per_device,
        mesh=mesh,
        in_specs=placed,
        out_specs=(P("feat", "dom"), P("feat", "dom"), P(None, "feat"), P("feat")),
        check_vma=False,
    )
```
